256 devices in a mesh: ctx: 32 (over x_lo, z, core), exp: 8 (over y, x_hi).
Axes of the slice: x: 4 (x_hi: 2, x_lo: 2; x = x_hi * 2 + x_lo), y: 4, z: 8, core: 2. Of those that a mesh axis runs over, the one named last changes fastest.
Arguments:
- hidden: bfloat16 [8192, 2048], P(('ctx', 'exp')), may hold values from -1.5 to 1.5
- lengths: int32 [2], replicated, may hold values from 2048 to 4096, as said below
- routes: int32 [8192, 8], P(('ctx', 'exp')), may hold values from 0 to 127, all different within a row; in each aligned block of 32 rows (0 to 31, 32 to 63, ...) at most 4 rows name the same one
- gates: float32 [8192, 8], P(('ctx', 'exp')), may hold values from 0.05 to 0.5
- attn_gain: float32 [2048], replicated, may hold values from 0.25 to 1.75
- q_weight: bfloat16 [2048, 4096], P('ctx', 'exp'), may hold values from -0.125 to 0.125
- key_value_weight: bfloat16 [2048, 1024], P('ctx'), may hold values from -0.125 to 0.125
- q_gain: float32 [128], replicated, may hold values from 0.25 to 1.75
- k_gain: float32 [128], replicated, may hold values from 0.25 to 1.75
- o_weight: bfloat16 [4096, 2048], P('exp', 'ctx'), may hold values from -0.09375 to 0.09375
- moe_gain: float32 [2048], replicated, may hold values from 0.25 to 1.75
- expert_in: bfloat16 [256, 2048, 768], P(('ctx', 'exp')), may hold values from -0.125 to 0.125
- expert_out: bfloat16 [256, 384, 2048], P(('ctx', 'exp')), may hold values from -0.21875 to 0.21875
Outputs:
- new_hidden: bfloat16 [8192, 2048], P(('ctx', 'exp'))
- cache: bfloat16 [2, 8192, 512], P(None, 'ctx', 'exp')
The draws below stay inside these ranges and needn't reach their ends.
Inputs may be any that keep to these rules, and one draw needn't show every extreme that they name: `lengths`: one of the two prompts has exactly 4096 positions; the other has 2048 to 4096. `routes`: A row names 8 different experts. Within the 32 rows of each device (aligned blocks of rows) no expert is named more than 4 times, a bound that some block reaches.
All inputs are finite; a program needn't handle non-finite values.
Results may differ from the reference program's by a relative error of at most 0.02.
Values may be sent and summed in bfloat16 or wider, within the bound.
No kernel may reach another device: no remote copies, remote signals or barrier semaphores. Data moves between devices by JAX's collectives and lax.ppermute only.
A program may use at most 128 MiB of HBM per device.

```python
import math
import jax
import jax.numpy as jnp
import numpy as np
from jax import lax

MODEL_WIDTH = 2048
QUERY_HEADS = 32
KEY_VALUE_HEADS = 4
HEAD_SIZE = 128
EXPERTS = 128
TOP = 8
FF = 768
TOK_CTX = 256
PACKED_LENGTH = 8192
LMAX = 4096
TOK_DEV = 32
SLICES = 2
FFS = 384
CAP = 4
N_CTX = 32
N_EXP = 8


def draw_lengths(key, part):
    picker = jax.random.randint(jax.random.fold_in(key, 11), (), 0, 2)
    shorter = jax.random.randint(jax.random.fold_in(key, 12), (), LMAX // 2, LMAX + 1)
    first_len = jnp.where(picker == 0, LMAX, shorter)
    second_len = jnp.where(picker == 0, shorter, LMAX)
    return jnp.stack([first_len, second_len]).astype(jnp.int32)


def levels(key, shape, split, low, high):
    level, own = 1.0, jax.random.fold_in(key, 6)
    for position, blocks in split:
        heights = jnp.exp(jax.random.uniform(jax.random.fold_in(own, position), (blocks,), jnp.float32, low / len(split), high / len(split)))
        level = level * jnp.repeat(heights, shape[position] // blocks).reshape([-1 if axis == position else 1 for axis in range(len(shape))])
    return level


def shared_out(rng, own, number, rows, count, top, reach, slope):
    order = jax.random.permutation(rng, count)
    crowded, ordinary = load_shares(count, rows * top, reach, slope, True), load_shares(count, rows * top, reach, slope, False)
    places = jnp.arange(count)

    def named(sizes, offset_by):
        used = int((sizes > 0).sum())
        fixed = max(1, used // 4)
        shifted = fixed + (places - fixed + offset_by * (used - fixed)) % max(1, count - fixed)
        return jnp.zeros((count,), jnp.int32).at[order[jnp.where(places < fixed, places, shifted)]].set(jnp.asarray(sizes, jnp.int32))

    sizes = jnp.where(number % 4 == 0, named(crowded, number // 4), named(ordinary, number - number // 4 - 1))
    mixed = jax.random.permutation(jax.random.fold_in(own, 3), count)
    giver, receiver = mixed[0:count // 2 * 2:2], mixed[1:count // 2 * 2:2]
    slack = jnp.minimum(sizes[giver] - 1, reach - sizes[receiver]) // 2
    slack = jnp.where((giver == order[0]) | (receiver == order[0]) | (sizes[receiver] == 0), 0, jnp.maximum(slack, 0))
    shifted = jax.random.randint(jax.random.fold_in(own, 4), (count // 2,), 0, 1 << 20) % (slack + 1)
    sizes = sizes.at[giver].add(-shifted).at[receiver].add(shifted)
    labels = jnp.searchsorted(jnp.cumsum(sizes), jnp.arange(rows * top), side="right").astype(jnp.int32)
    table = labels.reshape(top, rows).T
    table = table[jax.random.permutation(jax.random.fold_in(own, 1), rows)]
    offset_by = jax.random.randint(jax.random.fold_in(own, 2), (rows, 1), 0, top)
    return jnp.take_along_axis(table, (jnp.arange(top)[None, :] + offset_by) % top, axis=1)


def load_shares(amount, total, most, lean, full):
    portions = [(1 << 20) // math.isqrt(rank ** lean) + 1 for rank in range(1, amount + 1)]
    largest = most if full else min(most, max(-(-total // amount), total * portions[0] // sum(portions)))
    least = 1 if total - largest >= amount - 1 else 0
    given, rest = [largest] + [least] * (amount - 1), total - largest - least * (amount - 1)
    while rest > 0:
        movable = [i for i in range(1, amount) if given[i] < largest] or [i for i in range(1, amount) if given[i] < most]
        pool, budget = sum([portions[i] for i in movable]), rest
        for i in movable:
            extra = min(most - given[i], max(1, budget * portions[i] // pool), rest)
            given[i] = given[i] + extra
            rest = rest - extra
    return np.array(given)


def normal_values(key, dims, deviation, most, shards=(), kind=jnp.bfloat16):
    array = deviation * jax.random.normal(key, dims, jnp.float32)
    if shards:
        array = array * levels(key, dims, shards, -0.22, 0.18)
    return jnp.clip(array, -most, most).astype(kind)


def setup_inputs(seed: int = 0) -> dict:
    key_list = jax.random.split(jax.random.key(seed), 14)
    hidden = normal_values(key_list[0], (PACKED_LENGTH, MODEL_WIDTH), 0.25, 1.5, ((0, 256),))
    lengths = draw_lengths(jax.random.fold_in(key_list[13], 71), 0)
    routes_keys = jax.random.split(jax.random.fold_in(key_list[2], 1), PACKED_LENGTH // TOK_DEV)
    routes_turns = jax.random.permutation(jax.random.fold_in(key_list[2], 3), PACKED_LENGTH // TOK_DEV)
    routes = jax.vmap(lambda own, number: shared_out(jax.random.fold_in(key_list[2], 2), own, number, TOK_DEV, EXPERTS, TOP, CAP, 2))(routes_keys, routes_turns).reshape((PACKED_LENGTH, TOP))
    gates = jnp.clip(jnp.exp(math.log(0.5) - 2.3025851 * jax.random.uniform(key_list[3], (PACKED_LENGTH, TOP), jnp.float32) ** levels(key_list[3], (PACKED_LENGTH, TOP), ((0, 256),), -0.2, 0.2)), 0.05, 0.5)
    attn_gain = jnp.clip(1.0 + 0.15 * jax.random.normal(key_list[4], (MODEL_WIDTH,), jnp.float32), 0.25, 1.75)
    q_weight = normal_values(key_list[5], (MODEL_WIDTH, QUERY_HEADS * HEAD_SIZE), MODEL_WIDTH ** -0.5, 0.125, ((0, 32), (1, 8)))
    key_value_weight = normal_values(key_list[6], (MODEL_WIDTH, 2 * KEY_VALUE_HEADS * HEAD_SIZE), MODEL_WIDTH ** -0.5, 0.125, ((0, 32),))
    q_gain = jnp.clip(1.0 + 0.15 * jax.random.normal(key_list[7], (HEAD_SIZE,), jnp.float32), 0.25, 1.75)
    k_gain = jnp.clip(1.0 + 0.15 * jax.random.normal(key_list[8], (HEAD_SIZE,), jnp.float32), 0.25, 1.75)
    o_weight = normal_values(key_list[9], (QUERY_HEADS * HEAD_SIZE, MODEL_WIDTH), (QUERY_HEADS * HEAD_SIZE) ** -0.5, 0.09375, ((0, 8), (1, 32)))
    moe_gain = jnp.clip(1.0 + 0.15 * jax.random.normal(key_list[10], (MODEL_WIDTH,), jnp.float32), 0.25, 1.75)
    expert_in = normal_values(key_list[11], (EXPERTS * SLICES, MODEL_WIDTH, 2 * FFS), MODEL_WIDTH ** -0.5, 0.125, ((0, 256),))
    expert_out = normal_values(key_list[12], (EXPERTS * SLICES, FFS, MODEL_WIDTH), FF ** -0.5, 0.21875, ((0, 256),))
    return dict(hidden=hidden, lengths=lengths, routes=routes, gates=gates, attn_gain=attn_gain, q_weight=q_weight, key_value_weight=key_value_weight, q_gain=q_gain, k_gain=k_gain, o_weight=o_weight, moe_gain=moe_gain, expert_in=expert_in, expert_out=expert_out)


epsilon = 1e-06
rope_base = 1000000.0

def rms_scale(values, gain):
    mean_square = lax.optimization_barrier(jnp.mean(values * values, axis=-1, keepdims=True))
    return values * lax.rsqrt(mean_square + epsilon) * gain

def mirrored_position(row_ids, count_ctx, tok_ctx):
    half_rows = tok_ctx // 2
    holder = row_ids // tok_ctx
    within = row_ids % tok_ctx
    block_no = jnp.where(within < half_rows, holder, 2 * count_ctx - 1 - holder)
    return (block_no * half_rows + within % half_rows).astype(jnp.int32)

def document_info(token_positions, lengths):
    first_end = lengths[0]
    second_end = lengths[0] + lengths[1]
    document = (token_positions >= first_end).astype(jnp.int32) + (token_positions >= second_end).astype(jnp.int32)
    doc_start = jnp.where(document == 0, 0, jnp.where(document == 1, first_end, second_end))
    return (document, (token_positions - doc_start).astype(jnp.int32))

def rotate(values, rope_pos):
    head_width = values.shape[-1]
    freq_ids = jnp.arange(head_width // 2, dtype=jnp.float32)
    inverse = rope_base ** (-2.0 * freq_ids / head_width)
    angles = rope_pos.astype(jnp.float32)[:, None] * inverse[None, :]
    cosine = jnp.cos(angles)[:, None, :]
    sine_part = jnp.sin(angles)[:, None, :]
    first_half = values[..., :head_width // 2]
    second_half = values[..., head_width // 2:]
    return jnp.concatenate([first_half * cosine - second_half * sine_part, second_half * cosine + first_half * sine_part], axis=-1)

def reference(hidden, lengths, routes, gates, attn_gain, q_weight, key_value_weight, q_gain, k_gain, o_weight, moe_gain, expert_in, expert_out):
    row_ids = jnp.arange(PACKED_LENGTH, dtype=jnp.int32)
    token_positions = mirrored_position(row_ids, N_CTX, TOK_CTX)
    document, rope_pos = document_info(token_positions, lengths)
    normed = rms_scale(hidden.astype(jnp.float32), attn_gain).astype(jnp.bfloat16)
    q_raw = jnp.dot(normed, q_weight, preferred_element_type=jnp.float32).reshape(PACKED_LENGTH, QUERY_HEADS, HEAD_SIZE)
    key_value_plain = jnp.dot(normed, key_value_weight, preferred_element_type=jnp.float32)
    key_unrotated = key_value_plain[:, :KEY_VALUE_HEADS * HEAD_SIZE].reshape(PACKED_LENGTH, KEY_VALUE_HEADS, HEAD_SIZE)
    queries = rotate(rms_scale(q_raw, q_gain), rope_pos).astype(jnp.bfloat16)
    key_row_block = rotate(rms_scale(key_unrotated, k_gain), rope_pos).astype(jnp.bfloat16)
    value_row_block = key_value_plain[:, KEY_VALUE_HEADS * HEAD_SIZE:].astype(jnp.bfloat16).reshape(PACKED_LENGTH, KEY_VALUE_HEADS, HEAD_SIZE)
    head_groups = QUERY_HEADS // KEY_VALUE_HEADS
    score_scale = HEAD_SIZE ** (-0.5)
    allowed = (document[:, None] == document[None, :]) & (token_positions[None, :] <= token_positions[:, None])

    def one_head(head_id):
        query = lax.dynamic_index_in_dim(queries, head_id, 1, keepdims=False)
        key_head = lax.dynamic_index_in_dim(key_row_block, head_id // head_groups, 1, keepdims=False)
        value_head = lax.dynamic_index_in_dim(value_row_block, head_id // head_groups, 1, keepdims=False)
        scores = jnp.dot(query, key_head.T, preferred_element_type=jnp.float32) * score_scale
        weights = jnp.where(allowed, jnp.exp(scores), 0.0).astype(jnp.bfloat16)
        totals = lax.optimization_barrier(jnp.sum(weights.astype(jnp.float32), axis=1))
        context = jnp.dot(weights, value_head, preferred_element_type=jnp.float32) / totals[:, None]
        return context.astype(jnp.bfloat16)
    contexts = lax.map(one_head, jnp.arange(QUERY_HEADS, dtype=jnp.int32))
    context_rows = jnp.transpose(contexts, (1, 0, 2)).reshape(PACKED_LENGTH, QUERY_HEADS * HEAD_SIZE)
    residual_mid = hidden.astype(jnp.float32) + jnp.dot(context_rows, o_weight, preferred_element_type=jnp.float32)
    moe_in = rms_scale(residual_mid, moe_gain).astype(jnp.bfloat16)
    inner = expert_in.reshape(EXPERTS, SLICES, MODEL_WIDTH, 2 * FFS)
    outer = expert_out.reshape(EXPERTS, SLICES, FFS, MODEL_WIDTH)
    most_rows = N_CTX * N_EXP * CAP

    def one_expert(moe_sum, expert_id):
        hits = routes == expert_id
        weight_row = lax.optimization_barrier(jnp.sum(jnp.where(hits, gates, 0.0), axis=1))
        chosen = jnp.any(hits, axis=1)
        index_rows = jnp.nonzero(chosen, size=most_rows, fill_value=0)[0].astype(jnp.int32)
        valid = (jnp.arange(most_rows, dtype=jnp.int32) < jnp.sum(chosen.astype(jnp.int32))).astype(jnp.float32)
        taken = moe_in[index_rows]
        w_inner = lax.dynamic_index_in_dim(inner, expert_id, 0, keepdims=False)
        w_outer = lax.dynamic_index_in_dim(outer, expert_id, 0, keepdims=False)
        gate_up = jnp.einsum('rd,sdf->srf', taken.astype(jnp.float32), w_inner.astype(jnp.float32))
        activated = (jax.nn.silu(gate_up[..., :FFS]) * gate_up[..., FFS:]).astype(jnp.bfloat16)
        produced = jnp.einsum('srf,sfd->srd', activated.astype(jnp.float32), w_outer.astype(jnp.float32)).astype(jnp.bfloat16)
        summed = lax.optimization_barrier(jnp.sum(produced.astype(jnp.float32), axis=0))
        contrib = summed * (weight_row[index_rows] * valid)[:, None]
        return (moe_sum.at[index_rows].add(contrib), None)
    moe_out, unused_tail = lax.scan(one_expert, jnp.zeros((PACKED_LENGTH, MODEL_WIDTH), jnp.float32), jnp.arange(EXPERTS, dtype=jnp.int32))
    new_hidden = (residual_mid + moe_out).astype(jnp.bfloat16)
    key_store_cache = jnp.zeros((PACKED_LENGTH, KEY_VALUE_HEADS * HEAD_SIZE), jnp.bfloat16).at[token_positions].set(key_row_block.reshape(PACKED_LENGTH, KEY_VALUE_HEADS * HEAD_SIZE))
    value_store_cache = jnp.zeros((PACKED_LENGTH, KEY_VALUE_HEADS * HEAD_SIZE), jnp.bfloat16).at[token_positions].set(value_row_block.reshape(PACKED_LENGTH, KEY_VALUE_HEADS * HEAD_SIZE))
    return (new_hidden, jnp.stack([key_store_cache, value_store_cache]))
```

```python
import jax
import jax.numpy as jnp
from jax import lax
from jax.sharding import PartitionSpec as P

MODEL_WIDTH = 2048
QUERY_HEADS = 32
KEY_VALUE_HEADS = 4
HEAD_SIZE = 128
EXPERTS = 128
TOP = 8


epsilon = 1e-06
rope_base = 1000000.0


def from_behind(block, axis, distance):
    devices = range(lax.axis_size(axis))
    route = [((i - distance) % len(devices), i) for i in devices]
    return lax.ppermute(block, axis, route)


def rms_scale(values, gain):
    mean_square = jnp.mean(values * values, axis=-1, keepdims=True)
    return values * lax.rsqrt(mean_square + epsilon) * gain


def mirrored_position(row_ids, count_ctx, tok_ctx):
    half_rows = tok_ctx // 2
    holder = row_ids // tok_ctx
    within = row_ids % tok_ctx
    block_no = jnp.where(within < half_rows, holder, 2 * count_ctx - 1 - holder)
    return block_no * half_rows + within % half_rows


def document_info(token_positions, lengths):
    first_end = lengths[0]
    second_end = lengths[0] + lengths[1]
    document = (token_positions >= first_end).astype(jnp.int32) + (
        token_positions >= second_end
    ).astype(jnp.int32)
    doc_start = jnp.where(document == 0, 0, jnp.where(document == 1, first_end, second_end))
    return (document, token_positions - doc_start)


def rotate(values, rope_pos):
    head_width = values.shape[-1]
    freq_ids = jnp.arange(head_width // 2, dtype=jnp.float32)
    inverse = rope_base ** (-2.0 * freq_ids / head_width)
    angles = rope_pos.astype(jnp.float32)[:, None] * inverse[None, :]
    cosine = jnp.cos(angles)[:, None, :]
    sine_part = jnp.sin(angles)[:, None, :]
    first_half = values[..., : head_width // 2]
    second_half = values[..., head_width // 2 :]
    return jnp.concatenate(
        [
            first_half * cosine - second_half * sine_part,
            second_half * cosine + first_half * sine_part,
        ],
        axis=-1,
    )


def shards(
    hidden,
    lengths,
    routes,
    gates,
    attn_gain,
    q_weight,
    key_value_weight,
    q_gain,
    k_gain,
    o_weight,
    moe_gain,
    expert_in,
    expert_out,
):
    count_ctx = lax.axis_size("ctx")
    expert_count = lax.axis_size("exp")
    my_ctx = lax.axis_index("ctx")
    my_exp = lax.axis_index("exp")
    tok_dev = hidden.shape[0]
    tok_ctx = tok_dev * expert_count
    half_rows = tok_ctx // 2
    head_groups = QUERY_HEADS // KEY_VALUE_HEADS
    q_dev = QUERY_HEADS // expert_count
    key_value_share = max(1, KEY_VALUE_HEADS // expert_count)
    group_dev = q_dev // key_value_share
    column_share = KEY_VALUE_HEADS * HEAD_SIZE // expert_count
    key_value_leading = my_exp * q_dev // head_groups
    col_offset = my_exp * column_share - key_value_leading * HEAD_SIZE
    score_scale = HEAD_SIZE ** (-0.5)
    query_pos = mirrored_position(
        my_ctx * tok_ctx + jnp.arange(tok_ctx, dtype=jnp.int32), count_ctx, tok_ctx
    )
    query_doc, query_rope = document_info(query_pos, lengths)
    normed_own = rms_scale(hidden.astype(jnp.float32), attn_gain).astype(jnp.bfloat16)
    normed = lax.all_gather(normed_own, "exp", axis=0, tiled=True)
    key_cols = lax.dynamic_slice_in_dim(
        key_value_weight, key_value_leading * HEAD_SIZE, key_value_share * HEAD_SIZE, 1
    )
    value_column_block = lax.dynamic_slice_in_dim(
        key_value_weight,
        KEY_VALUE_HEADS * HEAD_SIZE + key_value_leading * HEAD_SIZE,
        key_value_share * HEAD_SIZE,
        1,
    )
    kv_local = jnp.concatenate([key_cols, value_column_block], axis=1)
    q_width = q_dev * HEAD_SIZE
    weights_all = lax.all_gather(
        jnp.concatenate([q_weight, kv_local], axis=1), "ctx", axis=0, tiled=True
    )
    projected = jnp.dot(normed, weights_all, preferred_element_type=jnp.float32)
    q_raw = projected[:, :q_width]
    key_value_plain = projected[:, q_width:]
    queries = rotate(
        rms_scale(q_raw.reshape(tok_ctx, q_dev, HEAD_SIZE), q_gain), query_rope
    ).astype(jnp.bfloat16)
    key_row_block = rotate(
        rms_scale(
            key_value_plain[:, : key_value_share * HEAD_SIZE].reshape(
                tok_ctx, key_value_share, HEAD_SIZE
            ),
            k_gain,
        ),
        query_rope,
    ).astype(jnp.bfloat16)
    value_row_block = key_value_plain[:, key_value_share * HEAD_SIZE :].astype(jnp.bfloat16)
    key_values = jnp.stack(
        [key_row_block.reshape(tok_ctx, key_value_share * HEAD_SIZE), value_row_block]
    )
    query_groups = queries.reshape(tok_ctx, key_value_share, group_dev, HEAD_SIZE)

    def attend(state_now, block_kv, offset):
        length_now = block_kv.shape[1]
        key_pos = mirrored_position(
            offset + jnp.arange(length_now, dtype=jnp.int32), count_ctx, tok_ctx
        )
        key_doc, unused_rope = document_info(key_pos, lengths)
        allowed = (query_doc[:, None] == key_doc[None, :]) & (
            key_pos[None, :] <= query_pos[:, None]
        )
        key_part = block_kv[0].reshape(length_now, key_value_share, HEAD_SIZE)
        value_part = block_kv[1].reshape(length_now, key_value_share, HEAD_SIZE)
        scores = (
            jnp.einsum("qkgd,skd->kgqs", query_groups, key_part, preferred_element_type=jnp.float32)
            * score_scale
        )
        weights = jnp.where(allowed[None, None], jnp.exp(scores), 0.0).astype(jnp.bfloat16)
        numerator = state_now[0] + jnp.einsum(
            "kgqs,skd->qkgd", weights, value_part, preferred_element_type=jnp.float32
        )
        denominator = state_now[1] + jnp.sum(weights, axis=-1, dtype=jnp.float32)
        return (numerator, denominator) + tuple(state_now[2:])

    initial = (
        jnp.zeros((tok_ctx, key_value_share, group_dev, HEAD_SIZE), jnp.float32),
        jnp.zeros((key_value_share, group_dev, tok_ctx), jnp.float32),
    )
    every_kv = lax.all_gather(key_values, "ctx", axis=1, tiled=True)
    total_rows = every_kv.shape[1]
    chunk = min(1024, total_rows)

    def turn(step_no, state_now):
        block_kv = lax.dynamic_slice_in_dim(every_kv, step_no * chunk, chunk, 1)
        return attend(state_now, block_kv, step_no * chunk)

    final_state = lax.fori_loop(0, total_rows // chunk, turn, initial)
    context = (
        (final_state[0] / jnp.transpose(final_state[1], (2, 0, 1))[..., None])
        .astype(jnp.bfloat16)
        .reshape(tok_ctx, q_dev * HEAD_SIZE)
    )
    def block_start(block_no):
        holder = jnp.where(block_no < count_ctx, block_no, 2 * count_ctx - 1 - block_no)
        return holder * tok_ctx + jnp.where(block_no < count_ctx, 0, half_rows)

    first_part = lax.dynamic_slice(
        every_kv, (0, block_start(2 * my_ctx), col_offset), (2, half_rows, column_share)
    )
    second_part = lax.dynamic_slice(
        every_kv, (0, block_start(2 * my_ctx + 1), col_offset), (2, half_rows, column_share)
    )
    cache = jnp.concatenate([first_part, second_part], axis=1)
    attn_part = jnp.dot(
        context,
        lax.all_gather(o_weight, "ctx", axis=1, tiled=True),
        preferred_element_type=jnp.float32,
    )
    attn_own = lax.psum_scatter(
        attn_part.astype(jnp.bfloat16), "exp", scatter_dimension=0, tiled=True
    ).astype(jnp.float32)
    residual_mid = hidden.astype(jnp.float32) + attn_own
    moe_in = rms_scale(residual_mid, moe_gain).astype(jnp.bfloat16)
    devices = count_ctx * expert_count
    slices = max(1, devices // EXPERTS)
    rows_dev = expert_in.shape[0]
    ffs_dev = expert_out.shape[1]
    capacity = max(4, 2 * tok_dev * TOP // EXPERTS)
    route_ids = routes.reshape(-1)
    route_count = route_ids.shape[0]
    expert_hot = (route_ids[:, None] == jnp.arange(EXPERTS, dtype=jnp.int32)[None, :]).astype(
        jnp.int32
    )
    ranking = jnp.sum(jnp.cumsum(expert_hot, axis=0) * expert_hot, axis=1) - 1
    slot_ids = route_ids * capacity + ranking
    slot_hot = (
        slot_ids[:, None] == jnp.arange(EXPERTS * capacity, dtype=jnp.int32)[None, :]
    ).astype(jnp.bfloat16)
    token_hot = (
        (jnp.arange(route_count, dtype=jnp.int32) // TOP)[:, None]
        == jnp.arange(tok_dev, dtype=jnp.int32)[None, :]
    ).astype(jnp.bfloat16)
    placement_map = jnp.einsum(
        "rs,rt->st", slot_hot, token_hot, preferred_element_type=jnp.float32
    ).astype(jnp.bfloat16)
    outgoing = jnp.dot(placement_map, moe_in, preferred_element_type=jnp.float32).astype(
        jnp.bfloat16
    )
    experts_ctx = EXPERTS // count_ctx
    outgoing = outgoing.reshape(count_ctx, experts_ctx * capacity, MODEL_WIDTH)
    landed = lax.all_to_all(outgoing, "ctx", split_axis=0, concat_axis=0, tiled=True)
    landed = jnp.broadcast_to(
        landed.reshape(count_ctx, experts_ctx, 1, capacity, MODEL_WIDTH),
        (count_ctx, experts_ctx, slices, capacity, MODEL_WIDTH),
    ).reshape(count_ctx, expert_count, capacity, MODEL_WIDTH)
    arrived = lax.all_to_all(landed, "exp", split_axis=1, concat_axis=1, tiled=True)
    arrived = arrived.reshape(count_ctx, expert_count, rows_dev, capacity, MODEL_WIDTH)
    gate_up = jnp.einsum("abrcd,rdf->abrcf", arrived, expert_in, preferred_element_type=jnp.float32)
    activated = (jax.nn.silu(gate_up[..., :ffs_dev]) * gate_up[..., ffs_dev:]).astype(jnp.bfloat16)
    produced = jnp.einsum(
        "abrcf,rfd->abrcd", activated, expert_out, preferred_element_type=jnp.float32
    ).astype(jnp.bfloat16)
    produced = produced.reshape(count_ctx, expert_count, rows_dev * capacity, MODEL_WIDTH)
    came_back = lax.all_to_all(produced, "exp", split_axis=1, concat_axis=1, tiled=True)
    part_sum = jnp.sum(
        came_back.reshape(count_ctx, experts_ctx, slices, capacity, MODEL_WIDTH),
        axis=2,
        dtype=jnp.float32,
    ).astype(jnp.bfloat16)
    returned = lax.all_to_all(
        part_sum.reshape(count_ctx, experts_ctx * capacity, MODEL_WIDTH),
        "ctx",
        split_axis=0,
        concat_axis=0,
        tiled=True,
    )
    slice_sum = returned.reshape(EXPERTS * capacity, MODEL_WIDTH).astype(jnp.float32)
    gate_hot = slot_hot.astype(jnp.float32) * gates.reshape(-1)[:, None]
    combiner = jnp.einsum(
        "rs,rt->ts", gate_hot, token_hot.astype(jnp.float32), precision=lax.Precision.HIGHEST
    )
    moe_out = jnp.dot(combiner, slice_sum, precision=lax.Precision.HIGHEST)
    new_hidden = (residual_mid + moe_out).astype(jnp.bfloat16)
    return (new_hidden, cache)


def solution(mesh):
    in_specs = (
        P(("ctx", "exp"), None),
        P(),
        P(("ctx", "exp"), None),
        P(("ctx", "exp"), None),
        P(),
        P("ctx", "exp"),
        P("ctx", None),
        P(),
        P(),
        P("exp", "ctx"),
        P(),
        P(("ctx", "exp"), None, None),
        P(("ctx", "exp"), None, None),
    )
    out_specs = (P(("ctx", "exp"), None), P(None, "ctx", "exp"))
    return jax.shard_map(shards, mesh=mesh, in_specs=in_specs, out_specs=out_specs, check_vma=False)
```

```python
import jax
import jax.numpy as jnp
from jax import lax
from jax.sharding import PartitionSpec as P

MODEL_WIDTH = 2048
QUERY_HEADS = 32
KEY_VALUE_HEADS = 4
HEAD_SIZE = 128
EXPERTS = 128
TOP = 8


epsilon = 1e-06
rope_base = 1000000.0


def from_behind(block, axis, distance):
    devices = range(lax.axis_size(axis))
    route = [((i - distance) % len(devices), i) for i in devices]
    return lax.ppermute(block, axis, route)


def rms_scale(values, gain):
    mean_square = jnp.mean(values * values, axis=-1, keepdims=True)
    return values * lax.rsqrt(mean_square + epsilon) * gain


def mirrored_position(row_ids, count_ctx, tok_ctx):
    half_rows = tok_ctx // 2
    holder = row_ids // tok_ctx
    within = row_ids % tok_ctx
    block_no = jnp.where(within < half_rows, holder, 2 * count_ctx - 1 - holder)
    return block_no * half_rows + within % half_rows


def document_info(token_positions, lengths):
    first_end = lengths[0]
    second_end = lengths[0] + lengths[1]
    document = (token_positions >= first_end).astype(jnp.int32) + (
        token_positions >= second_end
    ).astype(jnp.int32)
    doc_start = jnp.where(document == 0, 0, jnp.where(document == 1, first_end, second_end))
    return (document, token_positions - doc_start)


def rotate(values, rope_pos):
    head_width = values.shape[-1]
    freq_ids = jnp.arange(head_width // 2, dtype=jnp.float32)
    inverse = rope_base ** (-2.0 * freq_ids / head_width)
    angles = rope_pos.astype(jnp.float32)[:, None] * inverse[None, :]
    cosine = jnp.cos(angles)[:, None, :]
    sine_part = jnp.sin(angles)[:, None, :]
    first_half = values[..., : head_width // 2]
    second_half = values[..., head_width // 2 :]
    return jnp.concatenate(
        [
            first_half * cosine - second_half * sine_part,
            second_half * cosine + first_half * sine_part,
        ],
        axis=-1,
    )


def shards(
    hidden,
    lengths,
    routes,
    gates,
    attn_gain,
    q_weight,
    key_value_weight,
    q_gain,
    k_gain,
    o_weight,
    moe_gain,
    expert_in,
    expert_out,
):
    count_ctx = lax.axis_size("ctx")
    expert_count = lax.axis_size("exp")
    my_ctx = lax.axis_index("ctx")
    my_exp = lax.axis_index("exp")
    tok_dev = hidden.shape[0]
    tok_ctx = tok_dev * expert_count
    half_rows = tok_ctx // 2
    head_groups = QUERY_HEADS // KEY_VALUE_HEADS
    q_dev = QUERY_HEADS // expert_count
    key_value_share = max(1, KEY_VALUE_HEADS // expert_count)
    group_dev = q_dev // key_value_share
    column_share = KEY_VALUE_HEADS * HEAD_SIZE // expert_count
    key_value_leading = my_exp * q_dev // head_groups
    col_offset = my_exp * column_share - key_value_leading * HEAD_SIZE
    score_scale = HEAD_SIZE ** (-0.5)
    query_pos = mirrored_position(
        my_ctx * tok_ctx + jnp.arange(tok_ctx, dtype=jnp.int32), count_ctx, tok_ctx
    )
    query_doc, query_rope = document_info(query_pos, lengths)
    normed_own = rms_scale(hidden.astype(jnp.float32), attn_gain).astype(jnp.bfloat16)
    normed = lax.all_to_all(
        jnp.broadcast_to(normed_own[None], (expert_count,) + normed_own.shape),
        "exp",
        split_axis=0,
        concat_axis=0,
        tiled=True,
    ).reshape(tok_ctx, MODEL_WIDTH)
    key_cols = lax.dynamic_slice_in_dim(
        key_value_weight, key_value_leading * HEAD_SIZE, key_value_share * HEAD_SIZE, 1
    )
    value_column_block = lax.dynamic_slice_in_dim(
        key_value_weight,
        KEY_VALUE_HEADS * HEAD_SIZE + key_value_leading * HEAD_SIZE,
        key_value_share * HEAD_SIZE,
        1,
    )
    kv_local = jnp.concatenate([key_cols, value_column_block], axis=1)
    q_width = q_dev * HEAD_SIZE
    weights_all = lax.all_gather(
        jnp.concatenate([q_weight, kv_local], axis=1), "ctx", axis=0, tiled=True
    )
    projected = jnp.dot(normed, weights_all, preferred_element_type=jnp.float32)
    q_raw = projected[:, :q_width]
    key_value_plain = projected[:, q_width:]
    queries = rotate(
        rms_scale(q_raw.reshape(tok_ctx, q_dev, HEAD_SIZE), q_gain), query_rope
    ).astype(jnp.bfloat16)
    key_row_block = rotate(
        rms_scale(
            key_value_plain[:, : key_value_share * HEAD_SIZE].reshape(
                tok_ctx, key_value_share, HEAD_SIZE
            ),
            k_gain,
        ),
        query_rope,
    ).astype(jnp.bfloat16)
    value_row_block = key_value_plain[:, key_value_share * HEAD_SIZE :].astype(jnp.bfloat16)
    key_values = jnp.stack(
        [key_row_block.reshape(tok_ctx, key_value_share * HEAD_SIZE), value_row_block]
    )
    query_groups = queries.reshape(tok_ctx, key_value_share, group_dev, HEAD_SIZE)

    def attend(state_now, block_kv, offset):
        length_now = block_kv.shape[1]
        key_pos = mirrored_position(
            offset + jnp.arange(length_now, dtype=jnp.int32), count_ctx, tok_ctx
        )
        key_doc, unused_rope = document_info(key_pos, lengths)
        allowed = (query_doc[:, None] == key_doc[None, :]) & (
            key_pos[None, :] <= query_pos[:, None]
        )
        key_part = block_kv[0].reshape(length_now, key_value_share, HEAD_SIZE)
        value_part = block_kv[1].reshape(length_now, key_value_share, HEAD_SIZE)
        scores = (
            jnp.einsum("qkgd,skd->kgqs", query_groups, key_part, preferred_element_type=jnp.float32)
            * score_scale
        )
        weights = jnp.where(allowed[None, None], jnp.exp(scores), 0.0).astype(jnp.bfloat16)
        numerator = state_now[0] + jnp.einsum(
            "kgqs,skd->qkgd", weights, value_part, preferred_element_type=jnp.float32
        )
        denominator = state_now[1] + jnp.sum(weights, axis=-1, dtype=jnp.float32)
        return (numerator, denominator) + tuple(state_now[2:])

    initial = (
        jnp.zeros((tok_ctx, key_value_share, group_dev, HEAD_SIZE), jnp.float32),
        jnp.zeros((key_value_share, group_dev, tok_ctx), jnp.float32),
    )
    pair = [(i, i ^ 1) for i in range(expert_count)]
    every_kv, partner_in, partner_out = lax.optimization_barrier(
        (
            lax.all_gather(key_values, "ctx", axis=1, tiled=True),
            lax.ppermute(expert_in, "exp", pair),
            lax.ppermute(expert_out, "exp", pair),
        )
    )
    total_rows = every_kv.shape[1]
    chunk = min(1024, total_rows)

    def turn(step_no, state_now):
        block_kv = lax.dynamic_slice_in_dim(every_kv, step_no * chunk, chunk, 1)
        return attend(state_now, block_kv, step_no * chunk)

    final_state = lax.fori_loop(0, total_rows // chunk, turn, initial)
    context = (
        (final_state[0] / jnp.transpose(final_state[1], (2, 0, 1))[..., None])
        .astype(jnp.bfloat16)
        .reshape(tok_ctx, q_dev * HEAD_SIZE)
    )
    def block_start(block_no):
        holder = jnp.where(block_no < count_ctx, block_no, 2 * count_ctx - 1 - block_no)
        return holder * tok_ctx + jnp.where(block_no < count_ctx, 0, half_rows)

    first_part = lax.dynamic_slice(
        every_kv, (0, block_start(2 * my_ctx), col_offset), (2, half_rows, column_share)
    )
    second_part = lax.dynamic_slice(
        every_kv, (0, block_start(2 * my_ctx + 1), col_offset), (2, half_rows, column_share)
    )
    cache = jnp.concatenate([first_part, second_part], axis=1)
    attn_part = jnp.dot(
        context,
        lax.all_gather(o_weight, "ctx", axis=1, tiled=True),
        preferred_element_type=jnp.float32,
    )
    attn_pieces = lax.all_to_all(
        attn_part.astype(jnp.bfloat16).reshape(expert_count, tok_dev, MODEL_WIDTH),
        "exp",
        split_axis=0,
        concat_axis=0,
        tiled=True,
    )
    attn_own = jnp.sum(attn_pieces, axis=0, dtype=jnp.float32)
    residual_mid = hidden.astype(jnp.float32) + attn_own
    moe_in = rms_scale(residual_mid, moe_gain).astype(jnp.bfloat16)
    devices = count_ctx * expert_count
    slices = max(1, devices // EXPERTS)
    rows_dev = expert_in.shape[0]
    ffs_dev = expert_out.shape[1]
    capacity = max(4, 2 * tok_dev * TOP // EXPERTS)
    route_ids = routes.reshape(-1)
    route_count = route_ids.shape[0]
    expert_hot = (route_ids[:, None] == jnp.arange(EXPERTS, dtype=jnp.int32)[None, :]).astype(
        jnp.int32
    )
    ranking = jnp.sum(jnp.cumsum(expert_hot, axis=0) * expert_hot, axis=1) - 1
    slot_ids = route_ids * capacity + ranking
    slot_hot = (
        slot_ids[:, None] == jnp.arange(EXPERTS * capacity, dtype=jnp.int32)[None, :]
    ).astype(jnp.bfloat16)
    token_hot = (
        (jnp.arange(route_count, dtype=jnp.int32) // TOP)[:, None]
        == jnp.arange(tok_dev, dtype=jnp.int32)[None, :]
    ).astype(jnp.bfloat16)
    placement_map = jnp.einsum(
        "rs,rt->st", slot_hot, token_hot, preferred_element_type=jnp.float32
    ).astype(jnp.bfloat16)
    outgoing = jnp.dot(placement_map, moe_in, preferred_element_type=jnp.float32).astype(
        jnp.bfloat16
    )
    experts_ctx = EXPERTS // count_ctx
    share = capacity // slices
    expert_in_both = jnp.concatenate([expert_in, partner_in], axis=0)
    expert_out_both = jnp.concatenate([expert_out, partner_out], axis=0)
    outgoing = outgoing.reshape(count_ctx, experts_ctx * capacity, MODEL_WIDTH)
    landed = lax.all_to_all(outgoing, "ctx", split_axis=0, concat_axis=0, tiled=True)
    landed = landed.reshape(count_ctx, expert_count, share, MODEL_WIDTH)
    arrived = lax.all_to_all(landed, "exp", split_axis=1, concat_axis=1, tiled=True)
    tokens_in = arrived.reshape(-1, MODEL_WIDTH)
    gate_up = jnp.einsum(
        "td,sdf->stf", tokens_in, expert_in_both, preferred_element_type=jnp.float32
    )
    activated = (jax.nn.silu(gate_up[..., :ffs_dev]) * gate_up[..., ffs_dev:]).astype(jnp.bfloat16)
    produced = jnp.einsum(
        "stf,sfd->std", activated, expert_out_both, preferred_element_type=jnp.float32
    ).astype(jnp.bfloat16)
    produced = (
        jnp.sum(produced, axis=0, dtype=jnp.float32)
        .astype(jnp.bfloat16)
        .reshape(count_ctx, expert_count, share, MODEL_WIDTH)
    )
    came_back = lax.all_to_all(produced, "exp", split_axis=1, concat_axis=1, tiled=True)
    returned = lax.all_to_all(
        came_back.reshape(count_ctx, experts_ctx * capacity, MODEL_WIDTH),
        "ctx",
        split_axis=0,
        concat_axis=0,
        tiled=True,
    )
    slice_sum = returned.reshape(EXPERTS * capacity, MODEL_WIDTH).astype(jnp.float32)
    gate_hot = slot_hot.astype(jnp.float32) * gates.reshape(-1)[:, None]
    combiner = jnp.einsum(
        "rs,rt->ts", gate_hot, token_hot.astype(jnp.float32), precision=lax.Precision.HIGHEST
    )
    moe_out = jnp.dot(combiner, slice_sum, precision=lax.Precision.HIGHEST)
    new_hidden = (residual_mid + moe_out).astype(jnp.bfloat16)
    return (new_hidden, cache)


def solution(mesh):
    in_specs = (
        P(("ctx", "exp"), None),
        P(),
        P(("ctx", "exp"), None),
        P(("ctx", "exp"), None),
        P(),
        P("ctx", "exp"),
        P("ctx", None),
        P(),
        P(),
        P("exp", "ctx"),
        P(),
        P(("ctx", "exp"), None, None),
        P(("ctx", "exp"), None, None),
    )
    out_specs = (P(("ctx", "exp"), None), P(None, "ctx", "exp"))
    return jax.shard_map(shards, mesh=mesh, in_specs=in_specs, out_specs=out_specs, check_vma=False)
```

```python
import jax
import jax.numpy as jnp
from jax import lax
from jax.sharding import PartitionSpec as P

MODEL_WIDTH = 2048
QUERY_HEADS = 32
KEY_VALUE_HEADS = 4
HEAD_SIZE = 128
EXPERTS = 128
TOP = 8


epsilon = 1e-06
rope_base = 1000000.0


def from_behind(block, axis, distance):
    devices = range(lax.axis_size(axis))
    route = [((i - distance) % len(devices), i) for i in devices]
    return lax.ppermute(block, axis, route)


def rms_scale(values, gain):
    mean_square = jnp.mean(values * values, axis=-1, keepdims=True)
    return values * lax.rsqrt(mean_square + epsilon) * gain


def mirrored_position(row_ids, count_ctx, tok_ctx):
    half_rows = tok_ctx // 2
    holder = row_ids // tok_ctx
    within = row_ids % tok_ctx
    block_no = jnp.where(within < half_rows, holder, 2 * count_ctx - 1 - holder)
    return block_no * half_rows + within % half_rows


def document_info(token_positions, lengths):
    first_end = lengths[0]
    second_end = lengths[0] + lengths[1]
    document = (token_positions >= first_end).astype(jnp.int32) + (
        token_positions >= second_end
    ).astype(jnp.int32)
    doc_start = jnp.where(document == 0, 0, jnp.where(document == 1, first_end, second_end))
    return (document, token_positions - doc_start)


def rotate(values, rope_pos):
    head_width = values.shape[-1]
    freq_ids = jnp.arange(head_width // 2, dtype=jnp.float32)
    inverse = rope_base ** (-2.0 * freq_ids / head_width)
    angles = rope_pos.astype(jnp.float32)[:, None] * inverse[None, :]
    cosine = jnp.cos(angles)[:, None, :]
    sine_part = jnp.sin(angles)[:, None, :]
    first_half = values[..., : head_width // 2]
    second_half = values[..., head_width // 2 :]
    return jnp.concatenate(
        [
            first_half * cosine - second_half * sine_part,
            second_half * cosine + first_half * sine_part,
        ],
        axis=-1,
    )


def shards(
    hidden,
    lengths,
    routes,
    gates,
    attn_gain,
    q_weight,
    key_value_weight,
    q_gain,
    k_gain,
    o_weight,
    moe_gain,
    expert_in,
    expert_out,
):
    count_ctx = lax.axis_size("ctx")
    expert_count = lax.axis_size("exp")
    my_ctx = lax.axis_index("ctx")
    my_exp = lax.axis_index("exp")
    tok_dev = hidden.shape[0]
    tok_ctx = tok_dev * expert_count
    half_rows = tok_ctx // 2
    head_groups = QUERY_HEADS // KEY_VALUE_HEADS
    q_dev = QUERY_HEADS // expert_count
    key_value_share = max(1, KEY_VALUE_HEADS // expert_count)
    group_dev = q_dev // key_value_share
    column_share = KEY_VALUE_HEADS * HEAD_SIZE // expert_count
    key_value_leading = my_exp * q_dev // head_groups
    col_offset = my_exp * column_share - key_value_leading * HEAD_SIZE
    score_scale = HEAD_SIZE ** (-0.5)
    query_pos = mirrored_position(
        my_ctx * tok_ctx + jnp.arange(tok_ctx, dtype=jnp.int32), count_ctx, tok_ctx
    )
    query_doc, query_rope = document_info(query_pos, lengths)
    normed_own = rms_scale(hidden.astype(jnp.float32), attn_gain).astype(jnp.bfloat16)
    normed = lax.all_to_all(
        jnp.broadcast_to(normed_own[None], (expert_count,) + normed_own.shape),
        "exp",
        split_axis=0,
        concat_axis=0,
        tiled=True,
    ).reshape(tok_ctx, MODEL_WIDTH)
    key_cols = lax.dynamic_slice_in_dim(
        key_value_weight, key_value_leading * HEAD_SIZE, key_value_share * HEAD_SIZE, 1
    )
    value_column_block = lax.dynamic_slice_in_dim(
        key_value_weight,
        KEY_VALUE_HEADS * HEAD_SIZE + key_value_leading * HEAD_SIZE,
        key_value_share * HEAD_SIZE,
        1,
    )
    kv_local = jnp.concatenate([key_cols, value_column_block], axis=1)
    q_width = q_dev * HEAD_SIZE
    pair = [(i, i ^ 1) for i in range(expert_count)]
    rows_half = expert_in.shape[1] // 2
    weights_all, partner_out = lax.optimization_barrier(
        (
            lax.all_gather(
                jnp.concatenate([q_weight, kv_local], axis=1), "ctx", axis=0, tiled=True
            ),
            lax.ppermute(expert_out, "exp", pair),
        )
    )
    projected = jnp.dot(normed, weights_all, preferred_element_type=jnp.float32)
    q_raw = projected[:, :q_width]
    key_value_plain = projected[:, q_width:]
    queries = rotate(
        rms_scale(q_raw.reshape(tok_ctx, q_dev, HEAD_SIZE), q_gain), query_rope
    ).astype(jnp.bfloat16)
    key_row_block = rotate(
        rms_scale(
            key_value_plain[:, : key_value_share * HEAD_SIZE].reshape(
                tok_ctx, key_value_share, HEAD_SIZE
            ),
            k_gain,
        ),
        query_rope,
    ).astype(jnp.bfloat16)
    value_row_block = key_value_plain[:, key_value_share * HEAD_SIZE :].astype(jnp.bfloat16)
    key_values = jnp.stack(
        [key_row_block.reshape(tok_ctx, key_value_share * HEAD_SIZE), value_row_block]
    )
    query_groups = queries.reshape(tok_ctx, key_value_share, group_dev, HEAD_SIZE)

    def attend(state_now, block_kv, offset):
        length_now = block_kv.shape[1]
        key_pos = mirrored_position(
            offset + jnp.arange(length_now, dtype=jnp.int32), count_ctx, tok_ctx
        )
        key_doc, unused_rope = document_info(key_pos, lengths)
        allowed = (query_doc[:, None] == key_doc[None, :]) & (
            key_pos[None, :] <= query_pos[:, None]
        )
        key_part = block_kv[0].reshape(length_now, key_value_share, HEAD_SIZE)
        value_part = block_kv[1].reshape(length_now, key_value_share, HEAD_SIZE)
        scores = (
            jnp.einsum("qkgd,skd->kgqs", query_groups, key_part, preferred_element_type=jnp.float32)
            * score_scale
        )
        weights = jnp.where(allowed[None, None], jnp.exp(scores), 0.0).astype(jnp.bfloat16)
        numerator = state_now[0] + jnp.einsum(
            "kgqs,skd->qkgd", weights, value_part, preferred_element_type=jnp.float32
        )
        denominator = state_now[1] + jnp.sum(weights, axis=-1, dtype=jnp.float32)
        return (numerator, denominator) + tuple(state_now[2:])

    initial = (
        jnp.zeros((tok_ctx, key_value_share, group_dev, HEAD_SIZE), jnp.float32),
        jnp.zeros((key_value_share, group_dev, tok_ctx), jnp.float32),
    )
    every_kv, partner_in_low = lax.optimization_barrier(
        (
            lax.all_gather(key_values, "ctx", axis=1, tiled=True),
            lax.ppermute(expert_in[:, :rows_half], "exp", pair),
        )
    )
    total_rows = every_kv.shape[1]
    chunk = min(1024, total_rows)

    def turn(step_no, state_now):
        block_kv = lax.dynamic_slice_in_dim(every_kv, step_no * chunk, chunk, 1)
        return attend(state_now, block_kv, step_no * chunk)

    final_state, partner_in_high = lax.optimization_barrier(
        (
            lax.fori_loop(0, total_rows // chunk, turn, initial),
            lax.ppermute(expert_in[:, rows_half:], "exp", pair),
        )
    )
    context = (
        (final_state[0] / jnp.transpose(final_state[1], (2, 0, 1))[..., None])
        .astype(jnp.bfloat16)
        .reshape(tok_ctx, q_dev * HEAD_SIZE)
    )
    def block_start(block_no):
        holder = jnp.where(block_no < count_ctx, block_no, 2 * count_ctx - 1 - block_no)
        return holder * tok_ctx + jnp.where(block_no < count_ctx, 0, half_rows)

    first_part = lax.dynamic_slice(
        every_kv, (0, block_start(2 * my_ctx), col_offset), (2, half_rows, column_share)
    )
    second_part = lax.dynamic_slice(
        every_kv, (0, block_start(2 * my_ctx + 1), col_offset), (2, half_rows, column_share)
    )
    cache = jnp.concatenate([first_part, second_part], axis=1)
    attn_part = jnp.dot(
        context,
        lax.all_gather(o_weight, "ctx", axis=1, tiled=True),
        preferred_element_type=jnp.float32,
    )
    attn_pieces = lax.all_to_all(
        attn_part.astype(jnp.bfloat16).reshape(expert_count, tok_dev, MODEL_WIDTH),
        "exp",
        split_axis=0,
        concat_axis=0,
        tiled=True,
    )
    attn_own = jnp.sum(attn_pieces, axis=0, dtype=jnp.float32)
    residual_mid = hidden.astype(jnp.float32) + attn_own
    moe_in = rms_scale(residual_mid, moe_gain).astype(jnp.bfloat16)
    devices = count_ctx * expert_count
    slices = max(1, devices // EXPERTS)
    rows_dev = expert_in.shape[0]
    ffs_dev = expert_out.shape[1]
    capacity = max(4, 2 * tok_dev * TOP // EXPERTS)
    route_ids = routes.reshape(-1)
    route_count = route_ids.shape[0]
    expert_hot = (route_ids[:, None] == jnp.arange(EXPERTS, dtype=jnp.int32)[None, :]).astype(
        jnp.int32
    )
    ranking = jnp.sum(jnp.cumsum(expert_hot, axis=0) * expert_hot, axis=1) - 1
    slot_ids = route_ids * capacity + ranking
    slot_hot = (
        slot_ids[:, None] == jnp.arange(EXPERTS * capacity, dtype=jnp.int32)[None, :]
    ).astype(jnp.bfloat16)
    token_hot = (
        (jnp.arange(route_count, dtype=jnp.int32) // TOP)[:, None]
        == jnp.arange(tok_dev, dtype=jnp.int32)[None, :]
    ).astype(jnp.bfloat16)
    placement_map = jnp.einsum(
        "rs,rt->st", slot_hot, token_hot, preferred_element_type=jnp.float32
    ).astype(jnp.bfloat16)
    outgoing = jnp.dot(placement_map, moe_in, preferred_element_type=jnp.float32).astype(
        jnp.bfloat16
    )
    experts_ctx = EXPERTS // count_ctx
    share = capacity // slices
    partner_in = jnp.concatenate([partner_in_low, partner_in_high], axis=1)
    expert_in_both = jnp.concatenate([expert_in, partner_in], axis=0)
    expert_out_both = jnp.concatenate([expert_out, partner_out], axis=0)
    outgoing = outgoing.reshape(count_ctx, experts_ctx * capacity, MODEL_WIDTH)
    landed = lax.all_to_all(outgoing, "ctx", split_axis=0, concat_axis=0, tiled=True)
    landed = landed.reshape(count_ctx, expert_count, share, MODEL_WIDTH)
    arrived = lax.all_to_all(landed, "exp", split_axis=1, concat_axis=1, tiled=True)
    tokens_in = arrived.reshape(-1, MODEL_WIDTH)
    gate_up = jnp.einsum(
        "td,sdf->stf", tokens_in, expert_in_both, preferred_element_type=jnp.float32
    )
    activated = (jax.nn.silu(gate_up[..., :ffs_dev]) * gate_up[..., ffs_dev:]).astype(jnp.bfloat16)
    produced = jnp.einsum(
        "stf,sfd->std", activated, expert_out_both, preferred_element_type=jnp.float32
    ).astype(jnp.bfloat16)
    produced = (
        jnp.sum(produced, axis=0, dtype=jnp.float32)
        .astype(jnp.bfloat16)
        .reshape(count_ctx, expert_count, share, MODEL_WIDTH)
    )
    came_back = lax.all_to_all(produced, "exp", split_axis=1, concat_axis=1, tiled=True)
    returned = lax.all_to_all(
        came_back.reshape(count_ctx, experts_ctx * capacity, MODEL_WIDTH),
        "ctx",
        split_axis=0,
        concat_axis=0,
        tiled=True,
    )
    slice_sum = returned.reshape(EXPERTS * capacity, MODEL_WIDTH).astype(jnp.float32)
    gate_hot = slot_hot.astype(jnp.float32) * gates.reshape(-1)[:, None]
    combiner = jnp.einsum(
        "rs,rt->ts", gate_hot, token_hot.astype(jnp.float32), precision=lax.Precision.HIGHEST
    )
    moe_out = jnp.dot(combiner, slice_sum, precision=lax.Precision.HIGHEST)
    new_hidden = (residual_mid + moe_out).astype(jnp.bfloat16)
    return (new_hidden, cache)


def solution(mesh):
    in_specs = (
        P(("ctx", "exp"), None),
        P(),
        P(("ctx", "exp"), None),
        P(("ctx", "exp"), None),
        P(),
        P("ctx", "exp"),
        P("ctx", None),
        P(),
        P(),
        P("exp", "ctx"),
        P(),
        P(("ctx", "exp"), None, None),
        P(("ctx", "exp"), None, None),
    )
    out_specs = (P(("ctx", "exp"), None), P(None, "ctx", "exp"))
    return jax.shard_map(shards, mesh=mesh, in_specs=in_specs, out_specs=out_specs, check_vma=False)
```

```python
import jax
import jax.numpy as jnp
from jax import lax
from jax.sharding import PartitionSpec as P

MODEL_WIDTH = 2048
QUERY_HEADS = 32
KEY_VALUE_HEADS = 4
HEAD_SIZE = 128
EXPERTS = 128
TOP = 8


epsilon = 1e-06
rope_base = 1000000.0


def from_behind(block, axis, distance):
    devices = range(lax.axis_size(axis))
    route = [((i - distance) % len(devices), i) for i in devices]
    return lax.ppermute(block, axis, route)


def rms_scale(values, gain):
    mean_square = jnp.mean(values * values, axis=-1, keepdims=True)
    return values * lax.rsqrt(mean_square + epsilon) * gain


def mirrored_position(row_ids, count_ctx, tok_ctx):
    half_rows = tok_ctx // 2
    holder = row_ids // tok_ctx
    within = row_ids % tok_ctx
    block_no = jnp.where(within < half_rows, holder, 2 * count_ctx - 1 - holder)
    return block_no * half_rows + within % half_rows


def document_info(token_positions, lengths):
    first_end = lengths[0]
    second_end = lengths[0] + lengths[1]
    document = (token_positions >= first_end).astype(jnp.int32) + (
        token_positions >= second_end
    ).astype(jnp.int32)
    doc_start = jnp.where(document == 0, 0, jnp.where(document == 1, first_end, second_end))
    return (document, token_positions - doc_start)


def rotate(values, rope_pos):
    head_width = values.shape[-1]
    freq_ids = jnp.arange(head_width // 2, dtype=jnp.float32)
    inverse = rope_base ** (-2.0 * freq_ids / head_width)
    angles = rope_pos.astype(jnp.float32)[:, None] * inverse[None, :]
    cosine = jnp.cos(angles)[:, None, :]
    sine_part = jnp.sin(angles)[:, None, :]
    first_half = values[..., : head_width // 2]
    second_half = values[..., head_width // 2 :]
    return jnp.concatenate(
        [
            first_half * cosine - second_half * sine_part,
            second_half * cosine + first_half * sine_part,
        ],
        axis=-1,
    )


def shards(
    hidden,
    lengths,
    routes,
    gates,
    attn_gain,
    q_weight,
    key_value_weight,
    q_gain,
    k_gain,
    o_weight,
    moe_gain,
    expert_in,
    expert_out,
):
    count_ctx = lax.axis_size("ctx")
    expert_count = lax.axis_size("exp")
    my_ctx = lax.axis_index("ctx")
    my_exp = lax.axis_index("exp")
    tok_dev = hidden.shape[0]
    tok_ctx = tok_dev * expert_count
    half_rows = tok_ctx // 2
    head_groups = QUERY_HEADS // KEY_VALUE_HEADS
    q_dev = QUERY_HEADS // expert_count
    key_value_share = max(1, KEY_VALUE_HEADS // expert_count)
    group_dev = q_dev // key_value_share
    column_share = KEY_VALUE_HEADS * HEAD_SIZE // expert_count
    key_value_leading = my_exp * q_dev // head_groups
    col_offset = my_exp * column_share - key_value_leading * HEAD_SIZE
    score_scale = HEAD_SIZE ** (-0.5)
    query_pos = mirrored_position(
        my_ctx * tok_ctx + jnp.arange(tok_ctx, dtype=jnp.int32), count_ctx, tok_ctx
    )
    query_doc, query_rope = document_info(query_pos, lengths)
    normed_own = rms_scale(hidden.astype(jnp.float32), attn_gain).astype(jnp.bfloat16)
    normed = lax.all_to_all(
        jnp.broadcast_to(normed_own[None], (expert_count,) + normed_own.shape),
        "exp",
        split_axis=0,
        concat_axis=0,
        tiled=True,
    ).reshape(tok_ctx, MODEL_WIDTH)
    key_cols = lax.dynamic_slice_in_dim(
        key_value_weight, key_value_leading * HEAD_SIZE, key_value_share * HEAD_SIZE, 1
    )
    value_column_block = lax.dynamic_slice_in_dim(
        key_value_weight,
        KEY_VALUE_HEADS * HEAD_SIZE + key_value_leading * HEAD_SIZE,
        key_value_share * HEAD_SIZE,
        1,
    )
    kv_local = jnp.concatenate([key_cols, value_column_block], axis=1)
    q_width = q_dev * HEAD_SIZE
    pair = [(i, i ^ 1) for i in range(expert_count)]
    rows_half = expert_in.shape[1] // 2
    weights_all, partner_out = lax.optimization_barrier(
        (
            lax.all_gather(
                jnp.concatenate([q_weight, kv_local, o_weight.T], axis=1), "ctx", axis=0, tiled=True
            ),
            lax.ppermute(expert_out, "exp", pair),
        )
    )
    kv_width = kv_local.shape[1]
    projected = jnp.dot(
        normed, weights_all[:, : q_width + kv_width], preferred_element_type=jnp.float32
    )
    o_turned = weights_all[:, q_width + kv_width :]
    q_raw = projected[:, :q_width]
    key_value_plain = projected[:, q_width:]
    queries = rotate(
        rms_scale(q_raw.reshape(tok_ctx, q_dev, HEAD_SIZE), q_gain), query_rope
    ).astype(jnp.bfloat16)
    key_row_block = rotate(
        rms_scale(
            key_value_plain[:, : key_value_share * HEAD_SIZE].reshape(
                tok_ctx, key_value_share, HEAD_SIZE
            ),
            k_gain,
        ),
        query_rope,
    ).astype(jnp.bfloat16)
    value_row_block = key_value_plain[:, key_value_share * HEAD_SIZE :].astype(jnp.bfloat16)
    key_values = jnp.stack(
        [key_row_block.reshape(tok_ctx, key_value_share * HEAD_SIZE), value_row_block]
    )
    query_groups = queries.reshape(tok_ctx, key_value_share, group_dev, HEAD_SIZE)

    def attend(state_now, block_kv, offset):
        length_now = block_kv.shape[1]
        key_pos = mirrored_position(
            offset + jnp.arange(length_now, dtype=jnp.int32), count_ctx, tok_ctx
        )
        key_doc, unused_rope = document_info(key_pos, lengths)
        allowed = (query_doc[:, None] == key_doc[None, :]) & (
            key_pos[None, :] <= query_pos[:, None]
        )
        key_part = block_kv[0].reshape(length_now, key_value_share, HEAD_SIZE)
        value_part = block_kv[1].reshape(length_now, key_value_share, HEAD_SIZE)
        scores = (
            jnp.einsum("qkgd,skd->kgqs", query_groups, key_part, preferred_element_type=jnp.float32)
            * score_scale
        )
        weights = jnp.where(allowed[None, None], jnp.exp(scores), 0.0).astype(jnp.bfloat16)
        numerator = state_now[0] + jnp.einsum(
            "kgqs,skd->qkgd", weights, value_part, preferred_element_type=jnp.float32
        )
        denominator = state_now[1] + jnp.sum(weights, axis=-1, dtype=jnp.float32)
        return (numerator, denominator) + tuple(state_now[2:])

    initial = (
        jnp.zeros((tok_ctx, key_value_share, group_dev, HEAD_SIZE), jnp.float32),
        jnp.zeros((key_value_share, group_dev, tok_ctx), jnp.float32),
    )
    every_kv, partner_in_low = lax.optimization_barrier(
        (
            lax.all_gather(key_values, "ctx", axis=1, tiled=True),
            lax.ppermute(expert_in[:, :rows_half], "exp", pair),
        )
    )
    total_rows = every_kv.shape[1]
    chunk = min(1024, total_rows)

    def turn(step_no, state_now):
        block_kv = lax.dynamic_slice_in_dim(every_kv, step_no * chunk, chunk, 1)
        return attend(state_now, block_kv, step_no * chunk)

    final_state, partner_in_high = lax.optimization_barrier(
        (
            lax.fori_loop(0, total_rows // chunk, turn, initial),
            lax.ppermute(expert_in[:, rows_half:], "exp", pair),
        )
    )
    context = (
        (final_state[0] / jnp.transpose(final_state[1], (2, 0, 1))[..., None])
        .astype(jnp.bfloat16)
        .reshape(tok_ctx, q_dev * HEAD_SIZE)
    )
    def block_start(block_no):
        holder = jnp.where(block_no < count_ctx, block_no, 2 * count_ctx - 1 - block_no)
        return holder * tok_ctx + jnp.where(block_no < count_ctx, 0, half_rows)

    first_part = lax.dynamic_slice(
        every_kv, (0, block_start(2 * my_ctx), col_offset), (2, half_rows, column_share)
    )
    second_part = lax.dynamic_slice(
        every_kv, (0, block_start(2 * my_ctx + 1), col_offset), (2, half_rows, column_share)
    )
    cache = jnp.concatenate([first_part, second_part], axis=1)
    attn_part = lax.dot_general(
        context, o_turned, (((1,), (1,)), ((), ())), preferred_element_type=jnp.float32
    )
    attn_pieces = lax.all_to_all(
        attn_part.astype(jnp.bfloat16).reshape(expert_count, tok_dev, MODEL_WIDTH),
        "exp",
        split_axis=0,
        concat_axis=0,
        tiled=True,
    )
    attn_own = jnp.sum(attn_pieces, axis=0, dtype=jnp.float32)
    residual_mid = hidden.astype(jnp.float32) + attn_own
    moe_in = rms_scale(residual_mid, moe_gain).astype(jnp.bfloat16)
    devices = count_ctx * expert_count
    slices = max(1, devices // EXPERTS)
    rows_dev = expert_in.shape[0]
    ffs_dev = expert_out.shape[1]
    capacity = max(4, 2 * tok_dev * TOP // EXPERTS)
    route_ids = routes.reshape(-1)
    route_count = route_ids.shape[0]
    expert_hot = (route_ids[:, None] == jnp.arange(EXPERTS, dtype=jnp.int32)[None, :]).astype(
        jnp.int32
    )
    ranking = jnp.sum(jnp.cumsum(expert_hot, axis=0) * expert_hot, axis=1) - 1
    slot_ids = route_ids * capacity + ranking
    slot_hot = (
        slot_ids[:, None] == jnp.arange(EXPERTS * capacity, dtype=jnp.int32)[None, :]
    ).astype(jnp.bfloat16)
    token_hot = (
        (jnp.arange(route_count, dtype=jnp.int32) // TOP)[:, None]
        == jnp.arange(tok_dev, dtype=jnp.int32)[None, :]
    ).astype(jnp.bfloat16)
    placement_map = jnp.einsum(
        "rs,rt->st", slot_hot, token_hot, preferred_element_type=jnp.float32
    ).astype(jnp.bfloat16)
    outgoing = jnp.dot(placement_map, moe_in, preferred_element_type=jnp.float32).astype(
        jnp.bfloat16
    )
    experts_ctx = EXPERTS // count_ctx
    share = capacity // slices
    partner_in = jnp.concatenate([partner_in_low, partner_in_high], axis=1)
    expert_in_both = jnp.concatenate([expert_in, partner_in], axis=0)
    expert_out_both = jnp.concatenate([expert_out, partner_out], axis=0)
    outgoing = outgoing.reshape(devices, share, MODEL_WIDTH)
    arrived = lax.all_to_all(outgoing, ("ctx", "exp"), split_axis=0, concat_axis=0, tiled=True)
    tokens_in = arrived.reshape(-1, MODEL_WIDTH)
    gate_up = jnp.einsum(
        "td,sdf->stf", tokens_in, expert_in_both, preferred_element_type=jnp.float32
    )
    activated = (jax.nn.silu(gate_up[..., :ffs_dev]) * gate_up[..., ffs_dev:]).astype(jnp.bfloat16)
    produced = jnp.einsum(
        "stf,sfd->std", activated, expert_out_both, preferred_element_type=jnp.float32
    ).astype(jnp.bfloat16)
    produced = (
        jnp.sum(produced, axis=0, dtype=jnp.float32)
        .astype(jnp.bfloat16)
        .reshape(devices, share, MODEL_WIDTH)
    )
    returned = lax.all_to_all(produced, ("ctx", "exp"), split_axis=0, concat_axis=0, tiled=True)
    slice_sum = returned.reshape(EXPERTS * capacity, MODEL_WIDTH).astype(jnp.float32)
    gate_hot = slot_hot.astype(jnp.float32) * gates.reshape(-1)[:, None]
    combiner = jnp.einsum(
        "rs,rt->ts", gate_hot, token_hot.astype(jnp.float32), precision=lax.Precision.HIGHEST
    )
    moe_out = jnp.dot(combiner, slice_sum, precision=lax.Precision.HIGHEST)
    new_hidden = (residual_mid + moe_out).astype(jnp.bfloat16)
    return (new_hidden, cache)


def solution(mesh):
    in_specs = (
        P(("ctx", "exp"), None),
        P(),
        P(("ctx", "exp"), None),
        P(("ctx", "exp"), None),
        P(),
        P("ctx", "exp"),
        P("ctx", None),
        P(),
        P(),
        P("exp", "ctx"),
        P(),
        P(("ctx", "exp"), None, None),
        P(("ctx", "exp"), None, None),
    )
    out_specs = (P(("ctx", "exp"), None), P(None, "ctx", "exp"))
    return jax.shard_map(shards, mesh=mesh, in_specs=in_specs, out_specs=out_specs, check_vma=False)
```

```python
import jax
import jax.numpy as jnp
from jax import lax
from jax.sharding import PartitionSpec as P
from jax.experimental import pallas as pl
from jax.experimental.pallas import tpu as pltpu

MODEL_WIDTH = 2048
QUERY_HEADS = 32
KEY_VALUE_HEADS = 4
HEAD_SIZE = 128
EXPERTS = 128
TOP = 8


epsilon = 1e-06
rope_base = 1000000.0


def from_behind(block, axis, distance):
    devices = range(lax.axis_size(axis))
    route = [((i - distance) % len(devices), i) for i in devices]
    return lax.ppermute(block, axis, route)


def rms_scale(values, gain):
    mean_square = jnp.mean(values * values, axis=-1, keepdims=True)
    return values * lax.rsqrt(mean_square + epsilon) * gain


def mirrored_position(row_ids, count_ctx, tok_ctx):
    half_rows = tok_ctx // 2
    holder = row_ids // tok_ctx
    within = row_ids % tok_ctx
    block_no = jnp.where(within < half_rows, holder, 2 * count_ctx - 1 - holder)
    return block_no * half_rows + within % half_rows


def document_info(token_positions, lengths):
    first_end = lengths[0]
    second_end = lengths[0] + lengths[1]
    document = (token_positions >= first_end).astype(jnp.int32) + (
        token_positions >= second_end
    ).astype(jnp.int32)
    doc_start = jnp.where(document == 0, 0, jnp.where(document == 1, first_end, second_end))
    return (document, token_positions - doc_start)


def rotate(values, rope_pos):
    head_width = values.shape[-1]
    freq_ids = jnp.arange(head_width // 2, dtype=jnp.float32)
    inverse = rope_base ** (-2.0 * freq_ids / head_width)
    angles = rope_pos.astype(jnp.float32)[:, None] * inverse[None, :]
    cosine = jnp.cos(angles)[:, None, :]
    sine_part = jnp.sin(angles)[:, None, :]
    first_half = values[..., : head_width // 2]
    second_half = values[..., head_width // 2 :]
    return jnp.concatenate(
        [
            first_half * cosine - second_half * sine_part,
            second_half * cosine + first_half * sine_part,
        ],
        axis=-1,
    )


def attention_sums(q_rows, every_kv, q_pos, q_doc, k_pos, k_doc, scale, chunk):
    rows, width = q_rows.shape
    total = every_kv.shape[1]

    def body(q_ref, k_ref, v_ref, qp_ref, qd_ref, kp_ref, kd_ref, num_ref, den_ref):
        @pl.when(pl.program_id(0) == 0)
        def _():
            num_ref[...] = jnp.zeros_like(num_ref)
            den_ref[...] = jnp.zeros_like(den_ref)

        scores = (
            lax.dot_general(
                q_ref[...], k_ref[...], (((1,), (1,)), ((), ())),
                preferred_element_type=jnp.float32,
            )
            * scale
        )
        allowed = (qd_ref[...] == kd_ref[...]) & (kp_ref[...] <= qp_ref[...])
        weights = jnp.where(allowed, jnp.exp(scores), 0.0).astype(jnp.bfloat16)
        num_ref[...] += jnp.dot(weights, v_ref[...], preferred_element_type=jnp.float32)
        den_ref[...] += jnp.sum(weights.astype(jnp.float32), axis=1, keepdims=True)

    whole = lambda i: (0, 0)
    return pl.pallas_call(
        body,
        grid=(total // chunk,),
        in_specs=[
            pl.BlockSpec((rows, width), whole),
            pl.BlockSpec((None, chunk, width), lambda i: (0, i, 0)),
            pl.BlockSpec((None, chunk, width), lambda i: (1, i, 0)),
            pl.BlockSpec((rows, 1), whole),
            pl.BlockSpec((rows, 1), whole),
            pl.BlockSpec((1, chunk), lambda i: (0, i)),
            pl.BlockSpec((1, chunk), lambda i: (0, i)),
        ],
        out_specs=[pl.BlockSpec((rows, width), whole), pl.BlockSpec((rows, 1), whole)],
        out_shape=[
            jax.ShapeDtypeStruct((rows, width), jnp.float32),
            jax.ShapeDtypeStruct((rows, 1), jnp.float32),
        ],
        compiler_params=pltpu.CompilerParams(dimension_semantics=("arbitrary",)),
    )(q_rows, every_kv, every_kv, q_pos, q_doc, k_pos, k_doc)


def shards(
    hidden,
    lengths,
    routes,
    gates,
    attn_gain,
    q_weight,
    key_value_weight,
    q_gain,
    k_gain,
    o_weight,
    moe_gain,
    expert_in,
    expert_out,
):
    count_ctx = lax.axis_size("ctx")
    expert_count = lax.axis_size("exp")
    my_ctx = lax.axis_index("ctx")
    my_exp = lax.axis_index("exp")
    tok_dev = hidden.shape[0]
    tok_ctx = tok_dev * expert_count
    half_rows = tok_ctx // 2
    head_groups = QUERY_HEADS // KEY_VALUE_HEADS
    q_dev = QUERY_HEADS // expert_count
    key_value_share = max(1, KEY_VALUE_HEADS // expert_count)
    group_dev = q_dev // key_value_share
    column_share = KEY_VALUE_HEADS * HEAD_SIZE // expert_count
    key_value_leading = my_exp * q_dev // head_groups
    col_offset = my_exp * column_share - key_value_leading * HEAD_SIZE
    score_scale = HEAD_SIZE ** (-0.5)
    query_pos = mirrored_position(
        my_ctx * tok_ctx + jnp.arange(tok_ctx, dtype=jnp.int32), count_ctx, tok_ctx
    )
    query_doc, query_rope = document_info(query_pos, lengths)
    normed_own = rms_scale(hidden.astype(jnp.float32), attn_gain).astype(jnp.bfloat16)
    normed = lax.all_to_all(
        jnp.broadcast_to(normed_own[None], (expert_count,) + normed_own.shape),
        "exp",
        split_axis=0,
        concat_axis=0,
        tiled=True,
    ).reshape(tok_ctx, MODEL_WIDTH)
    key_cols = lax.dynamic_slice_in_dim(
        key_value_weight, key_value_leading * HEAD_SIZE, key_value_share * HEAD_SIZE, 1
    )
    value_column_block = lax.dynamic_slice_in_dim(
        key_value_weight,
        KEY_VALUE_HEADS * HEAD_SIZE + key_value_leading * HEAD_SIZE,
        key_value_share * HEAD_SIZE,
        1,
    )
    kv_local = jnp.concatenate([key_cols, value_column_block], axis=1)
    q_width = q_dev * HEAD_SIZE
    pair = [(i, i ^ 1) for i in range(expert_count)]
    rows_half = expert_in.shape[1] // 2
    weights_all, partner_out = lax.optimization_barrier(
        (
            lax.all_gather(
                jnp.concatenate([q_weight, kv_local, o_weight.T], axis=1), "ctx", axis=0, tiled=True
            ),
            lax.ppermute(expert_out, "exp", pair),
        )
    )
    kv_width = kv_local.shape[1]
    projected = jnp.dot(
        normed, weights_all[:, : q_width + kv_width], preferred_element_type=jnp.float32
    )
    o_turned = weights_all[:, q_width + kv_width :]
    q_raw = projected[:, :q_width]
    key_value_plain = projected[:, q_width:]
    queries = rotate(
        rms_scale(q_raw.reshape(tok_ctx, q_dev, HEAD_SIZE), q_gain), query_rope
    ).astype(jnp.bfloat16)
    key_row_block = rotate(
        rms_scale(
            key_value_plain[:, : key_value_share * HEAD_SIZE].reshape(
                tok_ctx, key_value_share, HEAD_SIZE
            ),
            k_gain,
        ),
        query_rope,
    ).astype(jnp.bfloat16)
    value_row_block = key_value_plain[:, key_value_share * HEAD_SIZE :].astype(jnp.bfloat16)
    key_values = jnp.stack(
        [key_row_block.reshape(tok_ctx, key_value_share * HEAD_SIZE), value_row_block]
    )

    every_kv, partner_in_low = lax.optimization_barrier(
        (
            lax.all_gather(key_values, "ctx", axis=1, tiled=True),
            lax.ppermute(expert_in[:, :rows_half], "exp", pair),
        )
    )
    total_rows = every_kv.shape[1]
    chunk = min(1024, total_rows)
    key_pos = mirrored_position(jnp.arange(total_rows, dtype=jnp.int32), count_ctx, tok_ctx)
    key_doc, unused_rope = document_info(key_pos, lengths)
    q_rows = jnp.transpose(queries, (1, 0, 2)).reshape(q_dev * tok_ctx, HEAD_SIZE)
    sums, partner_in_high = lax.optimization_barrier(
        (
            attention_sums(
                q_rows,
                every_kv,
                jnp.tile(query_pos, q_dev)[:, None],
                jnp.tile(query_doc, q_dev)[:, None],
                key_pos[None, :],
                key_doc[None, :],
                score_scale,
                chunk,
            ),
            lax.ppermute(expert_in[:, rows_half:], "exp", pair),
        )
    )
    numerator = jnp.transpose(sums[0].reshape(q_dev, tok_ctx, HEAD_SIZE), (1, 0, 2))
    denominator = jnp.transpose(sums[1].reshape(q_dev, tok_ctx, 1), (1, 0, 2))
    context = (numerator / denominator).astype(jnp.bfloat16).reshape(tok_ctx, q_dev * HEAD_SIZE)
    def block_start(block_no):
        holder = jnp.where(block_no < count_ctx, block_no, 2 * count_ctx - 1 - block_no)
        return holder * tok_ctx + jnp.where(block_no < count_ctx, 0, half_rows)

    first_part = lax.dynamic_slice(
        every_kv, (0, block_start(2 * my_ctx), col_offset), (2, half_rows, column_share)
    )
    second_part = lax.dynamic_slice(
        every_kv, (0, block_start(2 * my_ctx + 1), col_offset), (2, half_rows, column_share)
    )
    cache = jnp.concatenate([first_part, second_part], axis=1)
    attn_part = lax.dot_general(
        context, o_turned, (((1,), (1,)), ((), ())), preferred_element_type=jnp.float32
    )
    attn_pieces = lax.all_to_all(
        attn_part.astype(jnp.bfloat16).reshape(expert_count, tok_dev, MODEL_WIDTH),
        "exp",
        split_axis=0,
        concat_axis=0,
        tiled=True,
    )
    attn_own = jnp.sum(attn_pieces, axis=0, dtype=jnp.float32)
    residual_mid = hidden.astype(jnp.float32) + attn_own
    moe_in = rms_scale(residual_mid, moe_gain).astype(jnp.bfloat16)
    devices = count_ctx * expert_count
    slices = max(1, devices // EXPERTS)
    rows_dev = expert_in.shape[0]
    ffs_dev = expert_out.shape[1]
    capacity = max(4, 2 * tok_dev * TOP // EXPERTS)
    route_ids = routes.reshape(-1)
    route_count = route_ids.shape[0]
    expert_hot = (route_ids[:, None] == jnp.arange(EXPERTS, dtype=jnp.int32)[None, :]).astype(
        jnp.int32
    )
    ranking = jnp.sum(jnp.cumsum(expert_hot, axis=0) * expert_hot, axis=1) - 1
    slot_ids = route_ids * capacity + ranking
    slot_hot = (
        slot_ids[:, None] == jnp.arange(EXPERTS * capacity, dtype=jnp.int32)[None, :]
    ).astype(jnp.bfloat16)
    token_hot = (
        (jnp.arange(route_count, dtype=jnp.int32) // TOP)[:, None]
        == jnp.arange(tok_dev, dtype=jnp.int32)[None, :]
    ).astype(jnp.bfloat16)
    placement_map = jnp.einsum(
        "rs,rt->st", slot_hot, token_hot, preferred_element_type=jnp.float32
    ).astype(jnp.bfloat16)
    outgoing = jnp.dot(placement_map, moe_in, preferred_element_type=jnp.float32).astype(
        jnp.bfloat16
    )
    experts_ctx = EXPERTS // count_ctx
    share = capacity // slices
    partner_in = jnp.concatenate([partner_in_low, partner_in_high], axis=1)
    expert_in_both = jnp.concatenate([expert_in, partner_in], axis=0)
    expert_out_both = jnp.concatenate([expert_out, partner_out], axis=0)
    outgoing = outgoing.reshape(devices, share, MODEL_WIDTH)
    arrived = lax.all_to_all(outgoing, ("ctx", "exp"), split_axis=0, concat_axis=0, tiled=True)
    tokens_in = arrived.reshape(-1, MODEL_WIDTH)
    gate_up = jnp.einsum(
        "td,sdf->stf", tokens_in, expert_in_both, preferred_element_type=jnp.float32
    )
    activated = (jax.nn.silu(gate_up[..., :ffs_dev]) * gate_up[..., ffs_dev:]).astype(jnp.bfloat16)
    produced = jnp.einsum(
        "stf,sfd->std", activated, expert_out_both, preferred_element_type=jnp.float32
    ).astype(jnp.bfloat16)
    produced = (
        jnp.sum(produced, axis=0, dtype=jnp.float32)
        .astype(jnp.bfloat16)
        .reshape(devices, share, MODEL_WIDTH)
    )
    returned = lax.all_to_all(produced, ("ctx", "exp"), split_axis=0, concat_axis=0, tiled=True)
    slice_sum = returned.reshape(EXPERTS * capacity, MODEL_WIDTH).astype(jnp.float32)
    gate_hot = slot_hot.astype(jnp.float32) * gates.reshape(-1)[:, None]
    combiner = jnp.einsum(
        "rs,rt->ts", gate_hot, token_hot.astype(jnp.float32), precision=lax.Precision.HIGHEST
    )
    moe_out = jnp.dot(combiner, slice_sum, precision=lax.Precision.HIGHEST)
    new_hidden = (residual_mid + moe_out).astype(jnp.bfloat16)
    return (new_hidden, cache)


def solution(mesh):
    in_specs = (
        P(("ctx", "exp"), None),
        P(),
        P(("ctx", "exp"), None),
        P(("ctx", "exp"), None),
        P(),
        P("ctx", "exp"),
        P("ctx", None),
        P(),
        P(),
        P("exp", "ctx"),
        P(),
        P(("ctx", "exp"), None, None),
        P(("ctx", "exp"), None, None),
    )
    out_specs = (P(("ctx", "exp"), None), P(None, "ctx", "exp"))
    return jax.shard_map(shards, mesh=mesh, in_specs=in_specs, out_specs=out_specs, check_vma=False)
```

```python
import jax
import jax.numpy as jnp
from jax import lax
from jax.sharding import PartitionSpec as P
from jax.experimental import pallas as pl
from jax.experimental.pallas import tpu as pltpu

MODEL_WIDTH = 2048
QUERY_HEADS = 32
KEY_VALUE_HEADS = 4
HEAD_SIZE = 128
EXPERTS = 128
TOP = 8


epsilon = 1e-06
rope_base = 1000000.0


def from_behind(block, axis, distance):
    devices = range(lax.axis_size(axis))
    route = [((i - distance) % len(devices), i) for i in devices]
    return lax.ppermute(block, axis, route)


def rms_scale(values, gain):
    mean_square = jnp.mean(values * values, axis=-1, keepdims=True)
    return values * lax.rsqrt(mean_square + epsilon) * gain


def mirrored_position(row_ids, count_ctx, tok_ctx):
    half_rows = tok_ctx // 2
    holder = row_ids // tok_ctx
    within = row_ids % tok_ctx
    block_no = jnp.where(within < half_rows, holder, 2 * count_ctx - 1 - holder)
    return block_no * half_rows + within % half_rows


def document_info(token_positions, lengths):
    first_end = lengths[0]
    second_end = lengths[0] + lengths[1]
    document = (token_positions >= first_end).astype(jnp.int32) + (
        token_positions >= second_end
    ).astype(jnp.int32)
    doc_start = jnp.where(document == 0, 0, jnp.where(document == 1, first_end, second_end))
    return (document, token_positions - doc_start)


def rotate(values, rope_pos):
    head_width = values.shape[-1]
    freq_ids = jnp.arange(head_width // 2, dtype=jnp.float32)
    inverse = rope_base ** (-2.0 * freq_ids / head_width)
    angles = rope_pos.astype(jnp.float32)[:, None] * inverse[None, :]
    cosine = jnp.cos(angles)[:, None, :]
    sine_part = jnp.sin(angles)[:, None, :]
    first_half = values[..., : head_width // 2]
    second_half = values[..., head_width // 2 :]
    return jnp.concatenate(
        [
            first_half * cosine - second_half * sine_part,
            second_half * cosine + first_half * sine_part,
        ],
        axis=-1,
    )


def attention_sums(q_rows, every_kv, q_pos, q_doc, k_pos, k_doc, scale, chunk):
    rows, width = q_rows.shape
    total = every_kv.shape[1]

    def body(q_ref, k_ref, v_ref, qp_ref, qd_ref, kp_ref, kd_ref, num_ref, den_ref):
        @pl.when(pl.program_id(0) == 0)
        def _():
            num_ref[...] = jnp.zeros_like(num_ref)
            den_ref[...] = jnp.zeros_like(den_ref)

        scores = (
            lax.dot_general(
                q_ref[...], k_ref[...], (((1,), (1,)), ((), ())),
                preferred_element_type=jnp.float32,
            )
            * scale
        )
        allowed = (qd_ref[...] == kd_ref[...]) & (kp_ref[...] <= qp_ref[...])
        weights = jnp.where(allowed, jnp.exp(scores), 0.0).astype(jnp.bfloat16)
        num_ref[...] += jnp.dot(weights, v_ref[...], preferred_element_type=jnp.float32)
        den_ref[...] += jnp.sum(weights.astype(jnp.float32), axis=1, keepdims=True)

    whole = lambda i: (0, 0)
    return pl.pallas_call(
        body,
        grid=(total // chunk,),
        in_specs=[
            pl.BlockSpec((rows, width), whole),
            pl.BlockSpec((None, chunk, width), lambda i: (0, i, 0)),
            pl.BlockSpec((None, chunk, width), lambda i: (1, i, 0)),
            pl.BlockSpec((rows, 1), whole),
            pl.BlockSpec((rows, 1), whole),
            pl.BlockSpec((1, chunk), lambda i: (0, i)),
            pl.BlockSpec((1, chunk), lambda i: (0, i)),
        ],
        out_specs=[pl.BlockSpec((rows, width), whole), pl.BlockSpec((rows, 1), whole)],
        out_shape=[
            jax.ShapeDtypeStruct((rows, width), jnp.float32),
            jax.ShapeDtypeStruct((rows, 1), jnp.float32),
        ],
        compiler_params=pltpu.CompilerParams(dimension_semantics=("arbitrary",)),
    )(q_rows, every_kv, every_kv, q_pos, q_doc, k_pos, k_doc)


def shards(
    hidden,
    lengths,
    routes,
    gates,
    attn_gain,
    q_weight,
    key_value_weight,
    q_gain,
    k_gain,
    o_weight,
    moe_gain,
    expert_in,
    expert_out,
):
    count_ctx = lax.axis_size("ctx")
    expert_count = lax.axis_size("exp")
    my_ctx = lax.axis_index("ctx")
    my_exp = lax.axis_index("exp")
    tok_dev = hidden.shape[0]
    tok_ctx = tok_dev * expert_count
    half_rows = tok_ctx // 2
    head_groups = QUERY_HEADS // KEY_VALUE_HEADS
    q_dev = QUERY_HEADS // expert_count
    key_value_share = max(1, KEY_VALUE_HEADS // expert_count)
    group_dev = q_dev // key_value_share
    column_share = KEY_VALUE_HEADS * HEAD_SIZE // expert_count
    key_value_leading = my_exp * q_dev // head_groups
    col_offset = my_exp * column_share - key_value_leading * HEAD_SIZE
    score_scale = HEAD_SIZE ** (-0.5)
    query_pos = mirrored_position(
        my_ctx * tok_ctx + jnp.arange(tok_ctx, dtype=jnp.int32), count_ctx, tok_ctx
    )
    query_doc, query_rope = document_info(query_pos, lengths)
    normed_own = rms_scale(hidden.astype(jnp.float32), attn_gain).astype(jnp.bfloat16)
    normed = lax.all_to_all(
        jnp.broadcast_to(normed_own[None], (expert_count,) + normed_own.shape),
        "exp",
        split_axis=0,
        concat_axis=0,
        tiled=True,
    ).reshape(tok_ctx, MODEL_WIDTH)
    key_cols = lax.dynamic_slice_in_dim(
        key_value_weight, key_value_leading * HEAD_SIZE, key_value_share * HEAD_SIZE, 1
    )
    value_column_block = lax.dynamic_slice_in_dim(
        key_value_weight,
        KEY_VALUE_HEADS * HEAD_SIZE + key_value_leading * HEAD_SIZE,
        key_value_share * HEAD_SIZE,
        1,
    )
    kv_local = jnp.concatenate([key_cols, value_column_block], axis=1)
    q_width = q_dev * HEAD_SIZE
    pair = [(i, i ^ 1) for i in range(expert_count)]
    rows_half = expert_in.shape[1] // 2
    weights_all, partner_out = lax.optimization_barrier(
        (
            lax.all_gather(
                jnp.concatenate([q_weight, kv_local, o_weight.T], axis=1), "ctx", axis=0, tiled=True
            ),
            lax.ppermute(expert_out, "exp", pair),
        )
    )
    kv_width = kv_local.shape[1]
    projected = jnp.dot(
        normed, weights_all[:, : q_width + kv_width], preferred_element_type=jnp.float32
    )
    o_turned = weights_all[:, q_width + kv_width :]
    q_raw = projected[:, :q_width]
    key_value_plain = projected[:, q_width:]
    queries = rotate(
        rms_scale(q_raw.reshape(tok_ctx, q_dev, HEAD_SIZE), q_gain), query_rope
    ).astype(jnp.bfloat16)
    key_row_block = rotate(
        rms_scale(
            key_value_plain[:, : key_value_share * HEAD_SIZE].reshape(
                tok_ctx, key_value_share, HEAD_SIZE
            ),
            k_gain,
        ),
        query_rope,
    ).astype(jnp.bfloat16)
    value_row_block = key_value_plain[:, key_value_share * HEAD_SIZE :].astype(jnp.bfloat16)
    key_values = jnp.stack(
        [key_row_block.reshape(tok_ctx, key_value_share * HEAD_SIZE), value_row_block]
    )

    every_kv = lax.all_gather(key_values, "ctx", axis=1, tiled=True)
    total_rows = every_kv.shape[1]
    chunk = min(1024, total_rows)
    key_pos = mirrored_position(jnp.arange(total_rows, dtype=jnp.int32), count_ctx, tok_ctx)
    key_doc, unused_rope = document_info(key_pos, lengths)
    q_rows = jnp.transpose(queries, (1, 0, 2)).reshape(q_dev * tok_ctx, HEAD_SIZE)
    sums = attention_sums(
        q_rows,
        every_kv,
        jnp.tile(query_pos, q_dev)[:, None],
        jnp.tile(query_doc, q_dev)[:, None],
        key_pos[None, :],
        key_doc[None, :],
        score_scale,
        chunk,
    )
    numerator = jnp.transpose(sums[0].reshape(q_dev, tok_ctx, HEAD_SIZE), (1, 0, 2))
    denominator = jnp.transpose(sums[1].reshape(q_dev, tok_ctx, 1), (1, 0, 2))
    context = (numerator / denominator).astype(jnp.bfloat16).reshape(tok_ctx, q_dev * HEAD_SIZE)
    def block_start(block_no):
        holder = jnp.where(block_no < count_ctx, block_no, 2 * count_ctx - 1 - block_no)
        return holder * tok_ctx + jnp.where(block_no < count_ctx, 0, half_rows)

    first_part = lax.dynamic_slice(
        every_kv, (0, block_start(2 * my_ctx), col_offset), (2, half_rows, column_share)
    )
    second_part = lax.dynamic_slice(
        every_kv, (0, block_start(2 * my_ctx + 1), col_offset), (2, half_rows, column_share)
    )
    cache = jnp.concatenate([first_part, second_part], axis=1)
    attn_part = lax.dot_general(
        context, o_turned, (((1,), (1,)), ((), ())), preferred_element_type=jnp.float32
    )
    attn_pieces = lax.all_to_all(
        attn_part.astype(jnp.bfloat16).reshape(expert_count, tok_dev, MODEL_WIDTH),
        "exp",
        split_axis=0,
        concat_axis=0,
        tiled=True,
    )
    attn_pieces, partner_in_low, partner_in_high = lax.optimization_barrier(
        (
            attn_pieces,
            lax.ppermute(expert_in[:, :rows_half], "exp", pair),
            lax.ppermute(expert_in[:, rows_half:], "exp", pair),
        )
    )
    attn_own = jnp.sum(attn_pieces, axis=0, dtype=jnp.float32)
    residual_mid = hidden.astype(jnp.float32) + attn_own
    moe_in = rms_scale(residual_mid, moe_gain).astype(jnp.bfloat16)
    devices = count_ctx * expert_count
    slices = max(1, devices // EXPERTS)
    rows_dev = expert_in.shape[0]
    ffs_dev = expert_out.shape[1]
    capacity = max(4, 2 * tok_dev * TOP // EXPERTS)
    route_ids = routes.reshape(-1)
    route_count = route_ids.shape[0]
    expert_hot = (route_ids[:, None] == jnp.arange(EXPERTS, dtype=jnp.int32)[None, :]).astype(
        jnp.int32
    )
    ranking = jnp.sum(jnp.cumsum(expert_hot, axis=0) * expert_hot, axis=1) - 1
    slot_ids = route_ids * capacity + ranking
    slot_hot = (
        slot_ids[:, None] == jnp.arange(EXPERTS * capacity, dtype=jnp.int32)[None, :]
    ).astype(jnp.bfloat16)
    token_hot = (
        (jnp.arange(route_count, dtype=jnp.int32) // TOP)[:, None]
        == jnp.arange(tok_dev, dtype=jnp.int32)[None, :]
    ).astype(jnp.bfloat16)
    placement_map = jnp.einsum(
        "rs,rt->st", slot_hot, token_hot, preferred_element_type=jnp.float32
    ).astype(jnp.bfloat16)
    outgoing = jnp.dot(placement_map, moe_in, preferred_element_type=jnp.float32).astype(
        jnp.bfloat16
    )
    experts_ctx = EXPERTS // count_ctx
    share = capacity // slices
    partner_in = jnp.concatenate([partner_in_low, partner_in_high], axis=1)
    expert_in_both = jnp.concatenate([expert_in, partner_in], axis=0)
    expert_out_both = jnp.concatenate([expert_out, partner_out], axis=0)
    outgoing = outgoing.reshape(devices, share, MODEL_WIDTH)
    arrived = lax.all_to_all(outgoing, ("ctx", "exp"), split_axis=0, concat_axis=0, tiled=True)
    tokens_in = arrived.reshape(-1, MODEL_WIDTH)
    gate_up = jnp.einsum(
        "td,sdf->stf", tokens_in, expert_in_both, preferred_element_type=jnp.float32
    )
    activated = (jax.nn.silu(gate_up[..., :ffs_dev]) * gate_up[..., ffs_dev:]).astype(jnp.bfloat16)
    produced = jnp.einsum(
        "stf,sfd->std", activated, expert_out_both, preferred_element_type=jnp.float32
    ).astype(jnp.bfloat16)
    produced = (
        jnp.sum(produced, axis=0, dtype=jnp.float32)
        .astype(jnp.bfloat16)
        .reshape(devices, share, MODEL_WIDTH)
    )
    returned = lax.all_to_all(produced, ("ctx", "exp"), split_axis=0, concat_axis=0, tiled=True)
    slice_sum = returned.reshape(EXPERTS * capacity, MODEL_WIDTH).astype(jnp.float32)
    gate_hot = slot_hot.astype(jnp.float32) * gates.reshape(-1)[:, None]
    combiner = jnp.einsum(
        "rs,rt->ts", gate_hot, token_hot.astype(jnp.float32), precision=lax.Precision.HIGHEST
    )
    moe_out = jnp.dot(combiner, slice_sum, precision=lax.Precision.HIGHEST)
    new_hidden = (residual_mid + moe_out).astype(jnp.bfloat16)
    return (new_hidden, cache)


def solution(mesh):
    in_specs = (
        P(("ctx", "exp"), None),
        P(),
        P(("ctx", "exp"), None),
        P(("ctx", "exp"), None),
        P(),
        P("ctx", "exp"),
        P("ctx", None),
        P(),
        P(),
        P("exp", "ctx"),
        P(),
        P(("ctx", "exp"), None, None),
        P(("ctx", "exp"), None, None),
    )
    out_specs = (P(("ctx", "exp"), None), P(None, "ctx", "exp"))
    return jax.shard_map(shards, mesh=mesh, in_specs=in_specs, out_specs=out_specs, check_vma=False)
```

```python
import jax
import jax.numpy as jnp
from jax import lax
from jax.sharding import PartitionSpec as P
from jax.experimental import pallas as pl
from jax.experimental.pallas import tpu as pltpu

MODEL_WIDTH = 2048
QUERY_HEADS = 32
KEY_VALUE_HEADS = 4
HEAD_SIZE = 128
EXPERTS = 128
TOP = 8


epsilon = 1e-06
rope_base = 1000000.0


def from_behind(block, axis, distance):
    devices = range(lax.axis_size(axis))
    route = [((i - distance) % len(devices), i) for i in devices]
    return lax.ppermute(block, axis, route)


def rms_scale(values, gain):
    mean_square = jnp.mean(values * values, axis=-1, keepdims=True)
    return values * lax.rsqrt(mean_square + epsilon) * gain


def mirrored_position(row_ids, count_ctx, tok_ctx):
    half_rows = tok_ctx // 2
    holder = row_ids // tok_ctx
    within = row_ids % tok_ctx
    block_no = jnp.where(within < half_rows, holder, 2 * count_ctx - 1 - holder)
    return block_no * half_rows + within % half_rows


def document_info(token_positions, lengths):
    first_end = lengths[0]
    second_end = lengths[0] + lengths[1]
    document = (token_positions >= first_end).astype(jnp.int32) + (
        token_positions >= second_end
    ).astype(jnp.int32)
    doc_start = jnp.where(document == 0, 0, jnp.where(document == 1, first_end, second_end))
    return (document, token_positions - doc_start)


def rotate(values, rope_pos):
    head_width = values.shape[-1]
    freq_ids = jnp.arange(head_width // 2, dtype=jnp.float32)
    inverse = rope_base ** (-2.0 * freq_ids / head_width)
    angles = rope_pos.astype(jnp.float32)[:, None] * inverse[None, :]
    cosine = jnp.cos(angles)[:, None, :]
    sine_part = jnp.sin(angles)[:, None, :]
    first_half = values[..., : head_width // 2]
    second_half = values[..., head_width // 2 :]
    return jnp.concatenate(
        [
            first_half * cosine - second_half * sine_part,
            second_half * cosine + first_half * sine_part,
        ],
        axis=-1,
    )


def attention_sums(q_rows, every_kv, q_pos, q_doc, k_pos, k_doc, scale, chunk):
    rows, width = q_rows.shape
    total = every_kv.shape[1]

    def body(q_ref, k_ref, v_ref, qp_ref, qd_ref, kp_ref, kd_ref, num_ref, den_ref):
        @pl.when(pl.program_id(0) == 0)
        def _():
            num_ref[...] = jnp.zeros_like(num_ref)
            den_ref[...] = jnp.zeros_like(den_ref)

        scores = (
            lax.dot_general(
                q_ref[...], k_ref[...], (((1,), (1,)), ((), ())),
                preferred_element_type=jnp.float32,
            )
            * scale
        )
        allowed = (qd_ref[...] == kd_ref[...]) & (kp_ref[...] <= qp_ref[...])
        weights = jnp.where(allowed, jnp.exp(scores), 0.0).astype(jnp.bfloat16)
        values = v_ref[...]
        values_one = jnp.concatenate([values, jnp.ones_like(values)], axis=1)
        both = jnp.dot(weights, values_one, preferred_element_type=jnp.float32)
        num_ref[...] += both[:, :width]
        den_ref[...] += both[:, width : width + 1]

    whole = lambda i: (0, 0)
    return pl.pallas_call(
        body,
        grid=(total // chunk,),
        in_specs=[
            pl.BlockSpec((rows, width), whole),
            pl.BlockSpec((None, chunk, width), lambda i: (0, i, 0)),
            pl.BlockSpec((None, chunk, width), lambda i: (1, i, 0)),
            pl.BlockSpec((rows, 1), whole),
            pl.BlockSpec((rows, 1), whole),
            pl.BlockSpec((1, chunk), lambda i: (0, i)),
            pl.BlockSpec((1, chunk), lambda i: (0, i)),
        ],
        out_specs=[pl.BlockSpec((rows, width), whole), pl.BlockSpec((rows, 1), whole)],
        out_shape=[
            jax.ShapeDtypeStruct((rows, width), jnp.float32),
            jax.ShapeDtypeStruct((rows, 1), jnp.float32),
        ],
        compiler_params=pltpu.CompilerParams(dimension_semantics=("arbitrary",)),
    )(q_rows, every_kv, every_kv, q_pos, q_doc, k_pos, k_doc)


def shards(
    hidden,
    lengths,
    routes,
    gates,
    attn_gain,
    q_weight,
    key_value_weight,
    q_gain,
    k_gain,
    o_weight,
    moe_gain,
    expert_in,
    expert_out,
):
    count_ctx = lax.axis_size("ctx")
    expert_count = lax.axis_size("exp")
    my_ctx = lax.axis_index("ctx")
    my_exp = lax.axis_index("exp")
    tok_dev = hidden.shape[0]
    tok_ctx = tok_dev * expert_count
    half_rows = tok_ctx // 2
    head_groups = QUERY_HEADS // KEY_VALUE_HEADS
    q_dev = QUERY_HEADS // expert_count
    key_value_share = max(1, KEY_VALUE_HEADS // expert_count)
    group_dev = q_dev // key_value_share
    column_share = KEY_VALUE_HEADS * HEAD_SIZE // expert_count
    key_value_leading = my_exp * q_dev // head_groups
    col_offset = my_exp * column_share - key_value_leading * HEAD_SIZE
    score_scale = HEAD_SIZE ** (-0.5)
    query_pos = mirrored_position(
        my_ctx * tok_ctx + jnp.arange(tok_ctx, dtype=jnp.int32), count_ctx, tok_ctx
    )
    query_doc, query_rope = document_info(query_pos, lengths)
    normed_own = rms_scale(hidden.astype(jnp.float32), attn_gain).astype(jnp.bfloat16)
    normed = lax.all_to_all(
        jnp.broadcast_to(normed_own[None], (expert_count,) + normed_own.shape),
        "exp",
        split_axis=0,
        concat_axis=0,
        tiled=True,
    ).reshape(tok_ctx, MODEL_WIDTH)
    key_cols = lax.dynamic_slice_in_dim(
        key_value_weight, key_value_leading * HEAD_SIZE, key_value_share * HEAD_SIZE, 1
    )
    value_column_block = lax.dynamic_slice_in_dim(
        key_value_weight,
        KEY_VALUE_HEADS * HEAD_SIZE + key_value_leading * HEAD_SIZE,
        key_value_share * HEAD_SIZE,
        1,
    )
    kv_local = jnp.concatenate([key_cols, value_column_block], axis=1)
    q_width = q_dev * HEAD_SIZE
    pair = [(i, i ^ 1) for i in range(expert_count)]
    rows_half = expert_in.shape[1] // 2
    weights_all, partner_out = lax.optimization_barrier(
        (
            lax.all_gather(
                jnp.concatenate([q_weight, kv_local, o_weight.T], axis=1), "ctx", axis=0, tiled=True
            ),
            lax.ppermute(expert_out, "exp", pair),
        )
    )
    kv_width = kv_local.shape[1]
    projected = jnp.dot(
        normed, weights_all[:, : q_width + kv_width], preferred_element_type=jnp.float32
    )
    o_turned = weights_all[:, q_width + kv_width :]
    q_raw = projected[:, :q_width]
    key_value_plain = projected[:, q_width:]
    queries = rotate(
        rms_scale(q_raw.reshape(tok_ctx, q_dev, HEAD_SIZE), q_gain), query_rope
    ).astype(jnp.bfloat16)
    key_row_block = rotate(
        rms_scale(
            key_value_plain[:, : key_value_share * HEAD_SIZE].reshape(
                tok_ctx, key_value_share, HEAD_SIZE
            ),
            k_gain,
        ),
        query_rope,
    ).astype(jnp.bfloat16)
    value_row_block = key_value_plain[:, key_value_share * HEAD_SIZE :].astype(jnp.bfloat16)
    key_values = jnp.stack(
        [key_row_block.reshape(tok_ctx, key_value_share * HEAD_SIZE), value_row_block]
    )

    every_kv = lax.all_gather(key_values, "ctx", axis=1, tiled=True)
    total_rows = every_kv.shape[1]
    chunk = min(1024, total_rows)
    key_pos = mirrored_position(jnp.arange(total_rows, dtype=jnp.int32), count_ctx, tok_ctx)
    key_doc, unused_rope = document_info(key_pos, lengths)
    q_rows = jnp.transpose(queries, (1, 0, 2)).reshape(q_dev * tok_ctx, HEAD_SIZE)
    sums = attention_sums(
        q_rows,
        every_kv,
        jnp.tile(query_pos, q_dev)[:, None],
        jnp.tile(query_doc, q_dev)[:, None],
        key_pos[None, :],
        key_doc[None, :],
        score_scale,
        chunk,
    )
    numerator = jnp.transpose(sums[0].reshape(q_dev, tok_ctx, HEAD_SIZE), (1, 0, 2))
    denominator = jnp.transpose(sums[1].reshape(q_dev, tok_ctx, 1), (1, 0, 2))
    context = (numerator / denominator).astype(jnp.bfloat16).reshape(tok_ctx, q_dev * HEAD_SIZE)
    def block_start(block_no):
        holder = jnp.where(block_no < count_ctx, block_no, 2 * count_ctx - 1 - block_no)
        return holder * tok_ctx + jnp.where(block_no < count_ctx, 0, half_rows)

    first_part = lax.dynamic_slice(
        every_kv, (0, block_start(2 * my_ctx), col_offset), (2, half_rows, column_share)
    )
    second_part = lax.dynamic_slice(
        every_kv, (0, block_start(2 * my_ctx + 1), col_offset), (2, half_rows, column_share)
    )
    cache = jnp.concatenate([first_part, second_part], axis=1)
    attn_part = lax.dot_general(
        context, o_turned, (((1,), (1,)), ((), ())), preferred_element_type=jnp.float32
    )
    attn_pieces = lax.all_to_all(
        attn_part.astype(jnp.bfloat16).reshape(expert_count, tok_dev, MODEL_WIDTH),
        "exp",
        split_axis=0,
        concat_axis=0,
        tiled=True,
    )
    attn_pieces, partner_in_low, partner_in_high = lax.optimization_barrier(
        (
            attn_pieces,
            lax.ppermute(expert_in[:, :rows_half], "exp", pair),
            lax.ppermute(expert_in[:, rows_half:], "exp", pair),
        )
    )
    attn_own = jnp.sum(attn_pieces, axis=0, dtype=jnp.float32)
    residual_mid = hidden.astype(jnp.float32) + attn_own
    moe_in = rms_scale(residual_mid, moe_gain).astype(jnp.bfloat16)
    devices = count_ctx * expert_count
    slices = max(1, devices // EXPERTS)
    rows_dev = expert_in.shape[0]
    ffs_dev = expert_out.shape[1]
    capacity = max(4, 2 * tok_dev * TOP // EXPERTS)
    route_ids = routes.reshape(-1)
    route_count = route_ids.shape[0]
    expert_hot = (route_ids[:, None] == jnp.arange(EXPERTS, dtype=jnp.int32)[None, :]).astype(
        jnp.int32
    )
    ranking = jnp.sum(jnp.cumsum(expert_hot, axis=0) * expert_hot, axis=1) - 1
    slot_ids = route_ids * capacity + ranking
    slot_hot = (
        slot_ids[:, None] == jnp.arange(EXPERTS * capacity, dtype=jnp.int32)[None, :]
    ).astype(jnp.bfloat16)
    token_hot = (
        (jnp.arange(route_count, dtype=jnp.int32) // TOP)[:, None]
        == jnp.arange(tok_dev, dtype=jnp.int32)[None, :]
    ).astype(jnp.bfloat16)
    placement_map = jnp.einsum(
        "rs,rt->st", slot_hot, token_hot, preferred_element_type=jnp.float32
    ).astype(jnp.bfloat16)
    experts_ctx = EXPERTS // count_ctx
    share = capacity // slices
    outgoing = jnp.einsum(
        "dct,tf->dcf",
        placement_map.reshape(devices, share, tok_dev),
        moe_in,
        preferred_element_type=jnp.float32,
    ).astype(jnp.bfloat16)
    partner_in = jnp.concatenate([partner_in_low, partner_in_high], axis=1)
    expert_in_both = jnp.concatenate([expert_in, partner_in], axis=0)
    expert_out_both = jnp.concatenate([expert_out, partner_out], axis=0)
    arrived = lax.all_to_all(outgoing, ("ctx", "exp"), split_axis=0, concat_axis=0, tiled=True)
    gate_up = jnp.einsum(
        "dcf,sfh->sdch", arrived, expert_in_both, preferred_element_type=jnp.float32
    )
    activated = (jax.nn.silu(gate_up[..., :ffs_dev]) * gate_up[..., ffs_dev:]).astype(jnp.bfloat16)
    produced = jnp.einsum(
        "sdch,shf->sdcf", activated, expert_out_both, preferred_element_type=jnp.float32
    ).astype(jnp.bfloat16)
    produced = jnp.sum(produced, axis=0, dtype=jnp.float32).astype(jnp.bfloat16)
    returned = lax.all_to_all(produced, ("ctx", "exp"), split_axis=0, concat_axis=0, tiled=True)
    gate_hot = slot_hot.astype(jnp.float32) * gates.reshape(-1)[:, None]
    combiner = jnp.einsum(
        "rs,rt->ts", gate_hot, token_hot.astype(jnp.float32), precision=lax.Precision.HIGHEST
    )
    moe_out = jnp.einsum(
        "tdc,dcf->tf",
        combiner.reshape(tok_dev, devices, share),
        returned.astype(jnp.float32),
        precision=lax.Precision.HIGHEST,
    )
    new_hidden = (residual_mid + moe_out).astype(jnp.bfloat16)
    return (new_hidden, cache)


def solution(mesh):
    in_specs = (
        P(("ctx", "exp"), None),
        P(),
        P(("ctx", "exp"), None),
        P(("ctx", "exp"), None),
        P(),
        P("ctx", "exp"),
        P("ctx", None),
        P(),
        P(),
        P("exp", "ctx"),
        P(),
        P(("ctx", "exp"), None, None),
        P(("ctx", "exp"), None, None),
    )
    out_specs = (P(("ctx", "exp"), None), P(None, "ctx", "exp"))
    return jax.shard_map(shards, mesh=mesh, in_specs=in_specs, out_specs=out_specs, check_vma=False)
```

```python
import jax
import jax.numpy as jnp
from jax import lax
from jax.sharding import PartitionSpec as P
from jax.experimental import pallas as pl
from jax.experimental.pallas import tpu as pltpu

MODEL_WIDTH = 2048
QUERY_HEADS = 32
KEY_VALUE_HEADS = 4
HEAD_SIZE = 128
EXPERTS = 128
TOP = 8


epsilon = 1e-06
rope_base = 1000000.0


def from_behind(block, axis, distance):
    devices = range(lax.axis_size(axis))
    route = [((i - distance) % len(devices), i) for i in devices]
    return lax.ppermute(block, axis, route)


def rms_scale(values, gain):
    mean_square = jnp.mean(values * values, axis=-1, keepdims=True)
    return values * lax.rsqrt(mean_square + epsilon) * gain


def mirrored_position(row_ids, count_ctx, tok_ctx):
    half_rows = tok_ctx // 2
    holder = row_ids // tok_ctx
    within = row_ids % tok_ctx
    block_no = jnp.where(within < half_rows, holder, 2 * count_ctx - 1 - holder)
    return block_no * half_rows + within % half_rows


def document_info(token_positions, lengths):
    first_end = lengths[0]
    second_end = lengths[0] + lengths[1]
    document = (token_positions >= first_end).astype(jnp.int32) + (
        token_positions >= second_end
    ).astype(jnp.int32)
    doc_start = jnp.where(document == 0, 0, jnp.where(document == 1, first_end, second_end))
    return (document, token_positions - doc_start)


def rotate(values, rope_pos):
    head_width = values.shape[-1]
    freq_ids = jnp.arange(head_width // 2, dtype=jnp.float32)
    inverse = rope_base ** (-2.0 * freq_ids / head_width)
    angles = rope_pos.astype(jnp.float32)[:, None] * inverse[None, :]
    cosine = jnp.cos(angles)[:, None, :]
    sine_part = jnp.sin(angles)[:, None, :]
    first_half = values[..., : head_width // 2]
    second_half = values[..., head_width // 2 :]
    return jnp.concatenate(
        [
            first_half * cosine - second_half * sine_part,
            second_half * cosine + first_half * sine_part,
        ],
        axis=-1,
    )


def attention_context(q_rows, every_kv, q_pos, q_doc, k_pos, k_doc, scale, chunk, heads):
    rows, width = q_rows.shape
    tok = rows // heads
    total = every_kv.shape[1]
    steps = total // chunk

    def body(q_ref, k_ref, v_ref, qp_ref, qd_ref, kp_ref, kd_ref, out_ref, num_acc, den_acc):
        step = pl.program_id(0)

        @pl.when(step == 0)
        def _():
            num_acc[...] = jnp.zeros_like(num_acc)
            den_acc[...] = jnp.zeros_like(den_acc)

        scores = (
            lax.dot_general(
                q_ref[...], k_ref[...], (((1,), (1,)), ((), ())),
                preferred_element_type=jnp.float32,
            )
            * scale
        )
        allowed = (qd_ref[...] == kd_ref[...]) & (kp_ref[...] <= qp_ref[...])
        weights = jnp.where(allowed, jnp.exp(scores), 0.0).astype(jnp.bfloat16)
        values = v_ref[...]
        values_one = jnp.concatenate([values, jnp.ones_like(values)], axis=1)
        both = jnp.dot(weights, values_one, preferred_element_type=jnp.float32)
        num_acc[...] += both[:, :width]
        den_acc[...] += both[:, width : width + 1]

        @pl.when(step == steps - 1)
        def _():
            for head in range(heads):
                part = slice(head * tok, (head + 1) * tok)
                out_ref[:, head * width : (head + 1) * width] = (
                    num_acc[part, :] / den_acc[part, :]
                ).astype(out_ref.dtype)

    whole = lambda i: (0, 0)
    return pl.pallas_call(
        body,
        grid=(steps,),
        in_specs=[
            pl.BlockSpec((rows, width), whole),
            pl.BlockSpec((None, chunk, width), lambda i: (0, i, 0)),
            pl.BlockSpec((None, chunk, width), lambda i: (1, i, 0)),
            pl.BlockSpec((rows, 1), whole),
            pl.BlockSpec((rows, 1), whole),
            pl.BlockSpec((1, chunk), lambda i: (0, i)),
            pl.BlockSpec((1, chunk), lambda i: (0, i)),
        ],
        out_specs=pl.BlockSpec((tok, heads * width), whole),
        out_shape=jax.ShapeDtypeStruct((tok, heads * width), jnp.bfloat16),
        scratch_shapes=[pltpu.VMEM((rows, width), jnp.float32), pltpu.VMEM((rows, 1), jnp.float32)],
        compiler_params=pltpu.CompilerParams(dimension_semantics=("arbitrary",)),
    )(q_rows, every_kv, every_kv, q_pos, q_doc, k_pos, k_doc)


def shards(
    hidden,
    lengths,
    routes,
    gates,
    attn_gain,
    q_weight,
    key_value_weight,
    q_gain,
    k_gain,
    o_weight,
    moe_gain,
    expert_in,
    expert_out,
):
    count_ctx = lax.axis_size("ctx")
    expert_count = lax.axis_size("exp")
    my_ctx = lax.axis_index("ctx")
    my_exp = lax.axis_index("exp")
    tok_dev = hidden.shape[0]
    tok_ctx = tok_dev * expert_count
    half_rows = tok_ctx // 2
    head_groups = QUERY_HEADS // KEY_VALUE_HEADS
    q_dev = QUERY_HEADS // expert_count
    key_value_share = max(1, KEY_VALUE_HEADS // expert_count)
    group_dev = q_dev // key_value_share
    column_share = KEY_VALUE_HEADS * HEAD_SIZE // expert_count
    key_value_leading = my_exp * q_dev // head_groups
    col_offset = my_exp * column_share - key_value_leading * HEAD_SIZE
    score_scale = HEAD_SIZE ** (-0.5)
    query_pos = mirrored_position(
        my_ctx * tok_ctx + jnp.arange(tok_ctx, dtype=jnp.int32), count_ctx, tok_ctx
    )
    query_doc, query_rope = document_info(query_pos, lengths)
    normed_own = rms_scale(hidden.astype(jnp.float32), attn_gain).astype(jnp.bfloat16)
    normed = lax.all_to_all(
        jnp.broadcast_to(normed_own[None], (expert_count,) + normed_own.shape),
        "exp",
        split_axis=0,
        concat_axis=0,
        tiled=True,
    ).reshape(tok_ctx, MODEL_WIDTH)
    key_cols = lax.dynamic_slice_in_dim(
        key_value_weight, key_value_leading * HEAD_SIZE, key_value_share * HEAD_SIZE, 1
    )
    value_column_block = lax.dynamic_slice_in_dim(
        key_value_weight,
        KEY_VALUE_HEADS * HEAD_SIZE + key_value_leading * HEAD_SIZE,
        key_value_share * HEAD_SIZE,
        1,
    )
    kv_local = jnp.concatenate([key_cols, value_column_block], axis=1)
    q_width = q_dev * HEAD_SIZE
    pair = [(i, i ^ 1) for i in range(expert_count)]
    rows_half = expert_in.shape[1] // 2
    weights_all, partner_out = lax.optimization_barrier(
        (
            lax.all_gather(
                jnp.concatenate([q_weight, kv_local, o_weight.T], axis=1), "ctx", axis=0, tiled=True
            ),
            lax.ppermute(expert_out, "exp", pair),
        )
    )
    kv_width = kv_local.shape[1]
    projected = jnp.dot(
        normed, weights_all[:, : q_width + kv_width], preferred_element_type=jnp.float32
    )
    o_turned = weights_all[:, q_width + kv_width :]
    q_raw = projected[:, :q_width]
    key_value_plain = projected[:, q_width:]
    queries = rotate(
        rms_scale(q_raw.reshape(tok_ctx, q_dev, HEAD_SIZE), q_gain), query_rope
    ).astype(jnp.bfloat16)
    key_row_block = rotate(
        rms_scale(
            key_value_plain[:, : key_value_share * HEAD_SIZE].reshape(
                tok_ctx, key_value_share, HEAD_SIZE
            ),
            k_gain,
        ),
        query_rope,
    ).astype(jnp.bfloat16)
    value_row_block = key_value_plain[:, key_value_share * HEAD_SIZE :].astype(jnp.bfloat16)
    key_values = jnp.stack(
        [key_row_block.reshape(tok_ctx, key_value_share * HEAD_SIZE), value_row_block]
    )

    every_kv = lax.all_gather(key_values, "ctx", axis=1, tiled=True)
    total_rows = every_kv.shape[1]
    chunk = min(1024, total_rows)
    key_pos = mirrored_position(jnp.arange(total_rows, dtype=jnp.int32), count_ctx, tok_ctx)
    key_doc, unused_rope = document_info(key_pos, lengths)
    q_rows = jnp.transpose(queries, (1, 0, 2)).reshape(q_dev * tok_ctx, HEAD_SIZE)
    context = attention_context(
        q_rows,
        every_kv,
        jnp.tile(query_pos, q_dev)[:, None],
        jnp.tile(query_doc, q_dev)[:, None],
        key_pos[None, :],
        key_doc[None, :],
        score_scale,
        chunk,
        q_dev,
    )
    def block_start(block_no):
        holder = jnp.where(block_no < count_ctx, block_no, 2 * count_ctx - 1 - block_no)
        return holder * tok_ctx + jnp.where(block_no < count_ctx, 0, half_rows)

    first_part = lax.dynamic_slice(
        every_kv, (0, block_start(2 * my_ctx), col_offset), (2, half_rows, column_share)
    )
    second_part = lax.dynamic_slice(
        every_kv, (0, block_start(2 * my_ctx + 1), col_offset), (2, half_rows, column_share)
    )
    cache = jnp.concatenate([first_part, second_part], axis=1)
    attn_part = lax.dot_general(
        context, o_turned, (((1,), (1,)), ((), ())), preferred_element_type=jnp.float32
    )
    attn_pieces = lax.all_to_all(
        attn_part.astype(jnp.bfloat16).reshape(expert_count, tok_dev, MODEL_WIDTH),
        "exp",
        split_axis=0,
        concat_axis=0,
        tiled=True,
    )
    attn_pieces, partner_in_low, partner_in_high = lax.optimization_barrier(
        (
            attn_pieces,
            lax.ppermute(expert_in[:, :rows_half], "exp", pair),
            lax.ppermute(expert_in[:, rows_half:], "exp", pair),
        )
    )
    attn_own = jnp.sum(attn_pieces, axis=0, dtype=jnp.float32)
    residual_mid = hidden.astype(jnp.float32) + attn_own
    moe_in = rms_scale(residual_mid, moe_gain).astype(jnp.bfloat16)
    devices = count_ctx * expert_count
    slices = max(1, devices // EXPERTS)
    rows_dev = expert_in.shape[0]
    ffs_dev = expert_out.shape[1]
    capacity = max(4, 2 * tok_dev * TOP // EXPERTS)
    route_ids = routes.reshape(-1)
    route_count = route_ids.shape[0]
    expert_hot = (route_ids[:, None] == jnp.arange(EXPERTS, dtype=jnp.int32)[None, :]).astype(
        jnp.int32
    )
    ranking = jnp.sum(jnp.cumsum(expert_hot, axis=0) * expert_hot, axis=1) - 1
    slot_ids = route_ids * capacity + ranking
    slot_hot = (
        slot_ids[:, None] == jnp.arange(EXPERTS * capacity, dtype=jnp.int32)[None, :]
    ).astype(jnp.bfloat16)
    token_hot = (
        (jnp.arange(route_count, dtype=jnp.int32) // TOP)[:, None]
        == jnp.arange(tok_dev, dtype=jnp.int32)[None, :]
    ).astype(jnp.bfloat16)
    placement_map = jnp.einsum(
        "rs,rt->st", slot_hot, token_hot, preferred_element_type=jnp.float32
    ).astype(jnp.bfloat16)
    experts_ctx = EXPERTS // count_ctx
    share = capacity // slices
    outgoing = jnp.einsum(
        "dct,tf->dcf",
        placement_map.reshape(devices, share, tok_dev),
        moe_in,
        preferred_element_type=jnp.float32,
    ).astype(jnp.bfloat16)
    partner_in = jnp.concatenate([partner_in_low, partner_in_high], axis=1)
    expert_in_both = jnp.concatenate([expert_in, partner_in], axis=0)
    expert_out_both = jnp.concatenate([expert_out, partner_out], axis=0)
    arrived = lax.all_to_all(outgoing, ("ctx", "exp"), split_axis=0, concat_axis=0, tiled=True)
    gate_up = jnp.einsum(
        "dcf,sfh->sdch", arrived, expert_in_both, preferred_element_type=jnp.float32
    )
    activated = (jax.nn.silu(gate_up[..., :ffs_dev]) * gate_up[..., ffs_dev:]).astype(jnp.bfloat16)
    produced = jnp.einsum(
        "sdch,shf->sdcf", activated, expert_out_both, preferred_element_type=jnp.float32
    ).astype(jnp.bfloat16)
    produced = jnp.sum(produced, axis=0, dtype=jnp.float32).astype(jnp.bfloat16)
    returned = lax.all_to_all(produced, ("ctx", "exp"), split_axis=0, concat_axis=0, tiled=True)
    gate_hot = slot_hot.astype(jnp.float32) * gates.reshape(-1)[:, None]
    combiner = jnp.einsum(
        "rs,rt->ts", gate_hot, token_hot.astype(jnp.float32), precision=lax.Precision.HIGHEST
    )
    moe_out = jnp.einsum(
        "tdc,dcf->tf",
        combiner.reshape(tok_dev, devices, share),
        returned.astype(jnp.float32),
        precision=lax.Precision.HIGHEST,
    )
    new_hidden = (residual_mid + moe_out).astype(jnp.bfloat16)
    return (new_hidden, cache)


def solution(mesh):
    in_specs = (
        P(("ctx", "exp"), None),
        P(),
        P(("ctx", "exp"), None),
        P(("ctx", "exp"), None),
        P(),
        P("ctx", "exp"),
        P("ctx", None),
        P(),
        P(),
        P("exp", "ctx"),
        P(),
        P(("ctx", "exp"), None, None),
        P(("ctx", "exp"), None, None),
    )
    out_specs = (P(("ctx", "exp"), None), P(None, "ctx", "exp"))
    return jax.shard_map(shards, mesh=mesh, in_specs=in_specs, out_specs=out_specs, check_vma=False)
```

```python
import jax
import jax.numpy as jnp
from jax import lax
from jax.sharding import PartitionSpec as P
from jax.experimental import pallas as pl
from jax.experimental.pallas import tpu as pltpu

MODEL_WIDTH = 2048
QUERY_HEADS = 32
KEY_VALUE_HEADS = 4
HEAD_SIZE = 128
EXPERTS = 128
TOP = 8


epsilon = 1e-06
rope_base = 1000000.0


def from_behind(block, axis, distance):
    devices = range(lax.axis_size(axis))
    route = [((i - distance) % len(devices), i) for i in devices]
    return lax.ppermute(block, axis, route)


def rms_scale(values, gain):
    mean_square = jnp.mean(values * values, axis=-1, keepdims=True)
    return values * lax.rsqrt(mean_square + epsilon) * gain


def mirrored_position(row_ids, count_ctx, tok_ctx):
    half_rows = tok_ctx // 2
    holder = row_ids // tok_ctx
    within = row_ids % tok_ctx
    block_no = jnp.where(within < half_rows, holder, 2 * count_ctx - 1 - holder)
    return block_no * half_rows + within % half_rows


def document_info(token_positions, lengths):
    first_end = lengths[0]
    second_end = lengths[0] + lengths[1]
    document = (token_positions >= first_end).astype(jnp.int32) + (
        token_positions >= second_end
    ).astype(jnp.int32)
    doc_start = jnp.where(document == 0, 0, jnp.where(document == 1, first_end, second_end))
    return (document, token_positions - doc_start)


def rotate(values, rope_pos):
    head_width = values.shape[-1]
    freq_ids = jnp.arange(head_width // 2, dtype=jnp.float32)
    inverse = rope_base ** (-2.0 * freq_ids / head_width)
    angles = rope_pos.astype(jnp.float32)[:, None] * inverse[None, :]
    cosine = jnp.cos(angles)[:, None, :]
    sine_part = jnp.sin(angles)[:, None, :]
    first_half = values[..., : head_width // 2]
    second_half = values[..., head_width // 2 :]
    return jnp.concatenate(
        [
            first_half * cosine - second_half * sine_part,
            second_half * cosine + first_half * sine_part,
        ],
        axis=-1,
    )


def attention_context(q_rows, every_kv, q_pos, q_doc, k_pos, k_doc, scale, chunk, heads):
    rows, width = q_rows.shape
    tok = rows // heads
    total = every_kv.shape[1]
    steps = total // chunk

    def body(q_ref, k_ref, v_ref, qp_ref, qd_ref, kp_ref, kd_ref, out_ref, num_acc, den_acc):
        step = pl.program_id(0)

        @pl.when(step == 0)
        def _():
            num_acc[...] = jnp.zeros_like(num_acc)
            den_acc[...] = jnp.zeros_like(den_acc)

        scores = (
            lax.dot_general(
                q_ref[...], k_ref[...], (((1,), (1,)), ((), ())),
                preferred_element_type=jnp.float32,
            )
            * scale
        )
        allowed = (qd_ref[...] == kd_ref[...]) & (kp_ref[...] <= qp_ref[...])
        weights = jnp.where(allowed, jnp.exp(scores), 0.0).astype(jnp.bfloat16)
        values = v_ref[...]
        values_one = jnp.concatenate([values, jnp.ones_like(values)], axis=1)
        both = jnp.dot(weights, values_one, preferred_element_type=jnp.float32)
        num_acc[...] += both[:, :width]
        den_acc[...] += both[:, width : width + 1]

        @pl.when(step == steps - 1)
        def _():
            for head in range(heads):
                part = slice(head * tok, (head + 1) * tok)
                out_ref[:, head * width : (head + 1) * width] = (
                    num_acc[part, :] / den_acc[part, :]
                ).astype(out_ref.dtype)

    whole = lambda i: (0, 0)
    return pl.pallas_call(
        body,
        grid=(steps,),
        in_specs=[
            pl.BlockSpec((rows, width), whole),
            pl.BlockSpec((None, chunk, width), lambda i: (0, i, 0)),
            pl.BlockSpec((None, chunk, width), lambda i: (1, i, 0)),
            pl.BlockSpec((rows, 1), whole),
            pl.BlockSpec((rows, 1), whole),
            pl.BlockSpec((1, chunk), lambda i: (0, i)),
            pl.BlockSpec((1, chunk), lambda i: (0, i)),
        ],
        out_specs=pl.BlockSpec((tok, heads * width), whole),
        out_shape=jax.ShapeDtypeStruct((tok, heads * width), jnp.bfloat16),
        scratch_shapes=[pltpu.VMEM((rows, width), jnp.float32), pltpu.VMEM((rows, 1), jnp.float32)],
        compiler_params=pltpu.CompilerParams(dimension_semantics=("arbitrary",)),
    )(q_rows, every_kv, every_kv, q_pos, q_doc, k_pos, k_doc)


def shards(
    hidden,
    lengths,
    routes,
    gates,
    attn_gain,
    q_weight,
    key_value_weight,
    q_gain,
    k_gain,
    o_weight,
    moe_gain,
    expert_in,
    expert_out,
):
    count_ctx = lax.axis_size("ctx")
    expert_count = lax.axis_size("exp")
    my_ctx = lax.axis_index("ctx")
    my_exp = lax.axis_index("exp")
    tok_dev = hidden.shape[0]
    tok_ctx = tok_dev * expert_count
    half_rows = tok_ctx // 2
    head_groups = QUERY_HEADS // KEY_VALUE_HEADS
    q_dev = QUERY_HEADS // expert_count
    key_value_share = max(1, KEY_VALUE_HEADS // expert_count)
    group_dev = q_dev // key_value_share
    column_share = KEY_VALUE_HEADS * HEAD_SIZE // expert_count
    key_value_leading = my_exp * q_dev // head_groups
    col_offset = my_exp * column_share - key_value_leading * HEAD_SIZE
    score_scale = HEAD_SIZE ** (-0.5)
    query_pos = mirrored_position(
        my_ctx * tok_ctx + jnp.arange(tok_ctx, dtype=jnp.int32), count_ctx, tok_ctx
    )
    query_doc, query_rope = document_info(query_pos, lengths)
    normed_own = rms_scale(hidden.astype(jnp.float32), attn_gain).astype(jnp.bfloat16)
    normed = lax.all_to_all(
        jnp.broadcast_to(normed_own[None], (expert_count,) + normed_own.shape),
        "exp",
        split_axis=0,
        concat_axis=0,
        tiled=True,
    ).reshape(tok_ctx, MODEL_WIDTH)
    key_cols = lax.dynamic_slice_in_dim(
        key_value_weight, key_value_leading * HEAD_SIZE, key_value_share * HEAD_SIZE, 1
    )
    value_column_block = lax.dynamic_slice_in_dim(
        key_value_weight,
        KEY_VALUE_HEADS * HEAD_SIZE + key_value_leading * HEAD_SIZE,
        key_value_share * HEAD_SIZE,
        1,
    )
    kv_local = jnp.concatenate([key_cols, value_column_block], axis=1)
    q_width = q_dev * HEAD_SIZE
    pair = [(i, i ^ 1) for i in range(expert_count)]
    rows_half = expert_in.shape[1] // 2
    weights_all, partner_out = lax.optimization_barrier(
        (
            lax.all_gather(
                jnp.concatenate([q_weight, kv_local, o_weight.T], axis=1), "ctx", axis=0, tiled=True
            ),
            lax.ppermute(expert_out, "exp", pair),
        )
    )
    kv_width = kv_local.shape[1]
    projected = jnp.dot(
        normed, weights_all[:, : q_width + kv_width], preferred_element_type=jnp.float32
    )
    o_turned = weights_all[:, q_width + kv_width :]
    q_raw = projected[:, :q_width]
    key_value_plain = projected[:, q_width:]
    queries = rotate(
        rms_scale(q_raw.reshape(tok_ctx, q_dev, HEAD_SIZE), q_gain), query_rope
    ).astype(jnp.bfloat16)
    key_row_block = rotate(
        rms_scale(
            key_value_plain[:, : key_value_share * HEAD_SIZE].reshape(
                tok_ctx, key_value_share, HEAD_SIZE
            ),
            k_gain,
        ),
        query_rope,
    ).astype(jnp.bfloat16)
    value_row_block = key_value_plain[:, key_value_share * HEAD_SIZE :].astype(jnp.bfloat16)
    key_values = jnp.stack(
        [key_row_block.reshape(tok_ctx, key_value_share * HEAD_SIZE), value_row_block]
    )

    every_kv = lax.all_gather(key_values, "ctx", axis=1, tiled=True)
    total_rows = every_kv.shape[1]
    chunk = min(1024, total_rows)
    key_pos = mirrored_position(jnp.arange(total_rows, dtype=jnp.int32), count_ctx, tok_ctx)
    key_doc, unused_rope = document_info(key_pos, lengths)
    q_rows = jnp.transpose(queries, (1, 0, 2)).reshape(q_dev * tok_ctx, HEAD_SIZE)
    context = attention_context(
        q_rows,
        every_kv,
        jnp.tile(query_pos, q_dev)[:, None],
        jnp.tile(query_doc, q_dev)[:, None],
        key_pos[None, :],
        key_doc[None, :],
        score_scale,
        chunk,
        q_dev,
    )
    def block_start(block_no):
        holder = jnp.where(block_no < count_ctx, block_no, 2 * count_ctx - 1 - block_no)
        return holder * tok_ctx + jnp.where(block_no < count_ctx, 0, half_rows)

    first_part = lax.dynamic_slice(
        every_kv, (0, block_start(2 * my_ctx), col_offset), (2, half_rows, column_share)
    )
    second_part = lax.dynamic_slice(
        every_kv, (0, block_start(2 * my_ctx + 1), col_offset), (2, half_rows, column_share)
    )
    cache = jnp.concatenate([first_part, second_part], axis=1)
    attn_part = lax.dot_general(
        context, o_turned, (((1,), (1,)), ((), ())), preferred_element_type=jnp.float32
    )
    attn_pieces = lax.all_to_all(
        attn_part.astype(jnp.bfloat16).reshape(expert_count, tok_dev, MODEL_WIDTH),
        "exp",
        split_axis=0,
        concat_axis=0,
        tiled=True,
    )
    attn_pieces, partner_in_low = lax.optimization_barrier(
        (attn_pieces, lax.ppermute(expert_in[:, :rows_half], "exp", pair))
    )
    attn_own = jnp.sum(attn_pieces, axis=0, dtype=jnp.float32)
    residual_mid = hidden.astype(jnp.float32) + attn_own
    moe_in = rms_scale(residual_mid, moe_gain).astype(jnp.bfloat16)
    devices = count_ctx * expert_count
    slices = max(1, devices // EXPERTS)
    rows_dev = expert_in.shape[0]
    ffs_dev = expert_out.shape[1]
    capacity = max(4, 2 * tok_dev * TOP // EXPERTS)
    route_ids = routes.reshape(-1)
    route_count = route_ids.shape[0]
    expert_hot = (route_ids[:, None] == jnp.arange(EXPERTS, dtype=jnp.int32)[None, :]).astype(
        jnp.int32
    )
    ranking = jnp.sum(jnp.cumsum(expert_hot, axis=0) * expert_hot, axis=1) - 1
    slot_ids = route_ids * capacity + ranking
    slot_hot = (
        slot_ids[:, None] == jnp.arange(EXPERTS * capacity, dtype=jnp.int32)[None, :]
    ).astype(jnp.bfloat16)
    token_hot = (
        (jnp.arange(route_count, dtype=jnp.int32) // TOP)[:, None]
        == jnp.arange(tok_dev, dtype=jnp.int32)[None, :]
    ).astype(jnp.bfloat16)
    placement_map = jnp.einsum(
        "rs,rt->st", slot_hot, token_hot, preferred_element_type=jnp.float32
    ).astype(jnp.bfloat16)
    experts_ctx = EXPERTS // count_ctx
    share = capacity // slices
    outgoing = jnp.einsum(
        "dct,tf->dcf",
        placement_map.reshape(devices, share, tok_dev),
        moe_in,
        preferred_element_type=jnp.float32,
    ).astype(jnp.bfloat16)
    arrived, partner_in_high = lax.optimization_barrier(
        (
            lax.all_to_all(outgoing, ("ctx", "exp"), split_axis=0, concat_axis=0, tiled=True),
            lax.ppermute(expert_in[:, rows_half:], "exp", pair),
        )
    )
    partner_in = jnp.concatenate([partner_in_low, partner_in_high], axis=1)
    expert_in_both = jnp.concatenate([expert_in, partner_in], axis=0)
    expert_out_both = jnp.concatenate([expert_out, partner_out], axis=0)
    gate_up = jnp.einsum(
        "dcf,sfh->sdch", arrived, expert_in_both, preferred_element_type=jnp.float32
    )
    activated = (jax.nn.silu(gate_up[..., :ffs_dev]) * gate_up[..., ffs_dev:]).astype(jnp.bfloat16)
    produced = jnp.einsum(
        "sdch,shf->sdcf", activated, expert_out_both, preferred_element_type=jnp.float32
    ).astype(jnp.bfloat16)
    produced = jnp.sum(produced, axis=0, dtype=jnp.float32).astype(jnp.bfloat16)
    returned = lax.all_to_all(produced, ("ctx", "exp"), split_axis=0, concat_axis=0, tiled=True)
    gate_hot = slot_hot.astype(jnp.float32) * gates.reshape(-1)[:, None]
    combiner = jnp.einsum(
        "rs,rt->ts", gate_hot, token_hot.astype(jnp.float32), precision=lax.Precision.HIGHEST
    )
    moe_out = jnp.einsum(
        "tdc,dcf->tf",
        combiner.reshape(tok_dev, devices, share),
        returned.astype(jnp.float32),
        precision=lax.Precision.HIGHEST,
    )
    new_hidden = (residual_mid + moe_out).astype(jnp.bfloat16)
    return (new_hidden, cache)


def solution(mesh):
    in_specs = (
        P(("ctx", "exp"), None),
        P(),
        P(("ctx", "exp"), None),
        P(("ctx", "exp"), None),
        P(),
        P("ctx", "exp"),
        P("ctx", None),
        P(),
        P(),
        P("exp", "ctx"),
        P(),
        P(("ctx", "exp"), None, None),
        P(("ctx", "exp"), None, None),
    )
    out_specs = (P(("ctx", "exp"), None), P(None, "ctx", "exp"))
    return jax.shard_map(shards, mesh=mesh, in_specs=in_specs, out_specs=out_specs, check_vma=False)
```

```python
import jax
import jax.numpy as jnp
from jax import lax
from jax.sharding import PartitionSpec as P
from jax.experimental import pallas as pl
from jax.experimental.pallas import tpu as pltpu

MODEL_WIDTH = 2048
QUERY_HEADS = 32
KEY_VALUE_HEADS = 4
HEAD_SIZE = 128
EXPERTS = 128
TOP = 8


epsilon = 1e-06
rope_base = 1000000.0


def from_behind(block, axis, distance):
    devices = range(lax.axis_size(axis))
    route = [((i - distance) % len(devices), i) for i in devices]
    return lax.ppermute(block, axis, route)


def rms_scale(values, gain):
    mean_square = jnp.mean(values * values, axis=-1, keepdims=True)
    return values * lax.rsqrt(mean_square + epsilon) * gain


def mirrored_position(row_ids, count_ctx, tok_ctx):
    half_rows = tok_ctx // 2
    holder = row_ids // tok_ctx
    within = row_ids % tok_ctx
    block_no = jnp.where(within < half_rows, holder, 2 * count_ctx - 1 - holder)
    return block_no * half_rows + within % half_rows


def document_info(token_positions, lengths):
    first_end = lengths[0]
    second_end = lengths[0] + lengths[1]
    document = (token_positions >= first_end).astype(jnp.int32) + (
        token_positions >= second_end
    ).astype(jnp.int32)
    doc_start = jnp.where(document == 0, 0, jnp.where(document == 1, first_end, second_end))
    return (document, token_positions - doc_start)


def rotate(values, rope_pos):
    head_width = values.shape[-1]
    freq_ids = jnp.arange(head_width // 2, dtype=jnp.float32)
    inverse = rope_base ** (-2.0 * freq_ids / head_width)
    angles = rope_pos.astype(jnp.float32)[:, None] * inverse[None, :]
    cosine = jnp.cos(angles)[:, None, :]
    sine_part = jnp.sin(angles)[:, None, :]
    first_half = values[..., : head_width // 2]
    second_half = values[..., head_width // 2 :]
    return jnp.concatenate(
        [
            first_half * cosine - second_half * sine_part,
            second_half * cosine + first_half * sine_part,
        ],
        axis=-1,
    )


def attention_context(q_rows, every_kv, q_pos, q_doc, k_pos, k_doc, scale, chunk, heads):
    rows, width = q_rows.shape
    tok = rows // heads
    total = every_kv.shape[1]
    steps = total // chunk

    def body(q_ref, k_ref, v_ref, qp_ref, qd_ref, kp_ref, kd_ref, out_ref, num_acc, den_acc):
        step = pl.program_id(0)

        @pl.when(step == 0)
        def _():
            num_acc[...] = jnp.zeros_like(num_acc)
            den_acc[...] = jnp.zeros_like(den_acc)

        scores = (
            lax.dot_general(
                q_ref[...], k_ref[...], (((1,), (1,)), ((), ())),
                preferred_element_type=jnp.float32,
            )
            * scale
        )
        allowed = (qd_ref[...] == kd_ref[...]) & (kp_ref[...] <= qp_ref[...])
        weights = jnp.where(allowed, jnp.exp(scores), 0.0).astype(jnp.bfloat16)
        values = v_ref[...]
        values_one = jnp.concatenate([values, jnp.ones_like(values)], axis=1)
        both = jnp.dot(weights, values_one, preferred_element_type=jnp.float32)
        num_acc[...] += both[:, :width]
        den_acc[...] += both[:, width : width + 1]

        @pl.when(step == steps - 1)
        def _():
            for head in range(heads):
                part = slice(head * tok, (head + 1) * tok)
                out_ref[:, head * width : (head + 1) * width] = (
                    num_acc[part, :] / den_acc[part, :]
                ).astype(out_ref.dtype)

    whole = lambda i: (0, 0)
    return pl.pallas_call(
        body,
        grid=(steps,),
        in_specs=[
            pl.BlockSpec((rows, width), whole),
            pl.BlockSpec((None, chunk, width), lambda i: (0, i, 0)),
            pl.BlockSpec((None, chunk, width), lambda i: (1, i, 0)),
            pl.BlockSpec((rows, 1), whole),
            pl.BlockSpec((rows, 1), whole),
            pl.BlockSpec((1, chunk), lambda i: (0, i)),
            pl.BlockSpec((1, chunk), lambda i: (0, i)),
        ],
        out_specs=pl.BlockSpec((tok, heads * width), whole),
        out_shape=jax.ShapeDtypeStruct((tok, heads * width), jnp.bfloat16),
        scratch_shapes=[pltpu.VMEM((rows, width), jnp.float32), pltpu.VMEM((rows, 1), jnp.float32)],
        compiler_params=pltpu.CompilerParams(dimension_semantics=("arbitrary",)),
    )(q_rows, every_kv, every_kv, q_pos, q_doc, k_pos, k_doc)


def shards(
    hidden,
    lengths,
    routes,
    gates,
    attn_gain,
    q_weight,
    key_value_weight,
    q_gain,
    k_gain,
    o_weight,
    moe_gain,
    expert_in,
    expert_out,
):
    count_ctx = lax.axis_size("ctx")
    expert_count = lax.axis_size("exp")
    my_ctx = lax.axis_index("ctx")
    my_exp = lax.axis_index("exp")
    tok_dev = hidden.shape[0]
    tok_ctx = tok_dev * expert_count
    half_rows = tok_ctx // 2
    head_groups = QUERY_HEADS // KEY_VALUE_HEADS
    q_dev = QUERY_HEADS // expert_count
    key_value_share = max(1, KEY_VALUE_HEADS // expert_count)
    group_dev = q_dev // key_value_share
    column_share = KEY_VALUE_HEADS * HEAD_SIZE // expert_count
    key_value_leading = my_exp * q_dev // head_groups
    col_offset = my_exp * column_share - key_value_leading * HEAD_SIZE
    score_scale = HEAD_SIZE ** (-0.5)
    query_pos = mirrored_position(
        my_ctx * tok_ctx + jnp.arange(tok_ctx, dtype=jnp.int32), count_ctx, tok_ctx
    )
    query_doc, query_rope = document_info(query_pos, lengths)
    normed_own = rms_scale(hidden.astype(jnp.float32), attn_gain).astype(jnp.bfloat16)
    normed = lax.all_to_all(
        jnp.broadcast_to(normed_own[None], (expert_count,) + normed_own.shape),
        "exp",
        split_axis=0,
        concat_axis=0,
        tiled=True,
    ).reshape(tok_ctx, MODEL_WIDTH)
    key_cols = lax.dynamic_slice_in_dim(
        key_value_weight, key_value_leading * HEAD_SIZE, key_value_share * HEAD_SIZE, 1
    )
    value_column_block = lax.dynamic_slice_in_dim(
        key_value_weight,
        KEY_VALUE_HEADS * HEAD_SIZE + key_value_leading * HEAD_SIZE,
        key_value_share * HEAD_SIZE,
        1,
    )
    kv_local = jnp.concatenate([key_cols, value_column_block], axis=1)
    q_width = q_dev * HEAD_SIZE
    pair = [(i, i ^ 1) for i in range(expert_count)]
    rows_half = expert_in.shape[1] // 2
    weights_all, partner_out = lax.optimization_barrier(
        (
            lax.all_gather(
                jnp.concatenate([q_weight, kv_local, o_weight.T], axis=1), "ctx", axis=0, tiled=True
            ),
            lax.ppermute(expert_out, "exp", pair),
        )
    )
    kv_width = kv_local.shape[1]
    projected = jnp.dot(
        normed, weights_all[:, : q_width + kv_width], preferred_element_type=jnp.float32
    )
    o_turned = weights_all[:, q_width + kv_width :]
    q_raw = projected[:, :q_width]
    key_value_plain = projected[:, q_width:]
    queries = rotate(
        rms_scale(q_raw.reshape(tok_ctx, q_dev, HEAD_SIZE), q_gain), query_rope
    ).astype(jnp.bfloat16)
    key_row_block = rotate(
        rms_scale(
            key_value_plain[:, : key_value_share * HEAD_SIZE].reshape(
                tok_ctx, key_value_share, HEAD_SIZE
            ),
            k_gain,
        ),
        query_rope,
    ).astype(jnp.bfloat16)
    value_row_block = key_value_plain[:, key_value_share * HEAD_SIZE :].astype(jnp.bfloat16)
    key_values = jnp.stack(
        [key_row_block.reshape(tok_ctx, key_value_share * HEAD_SIZE), value_row_block]
    )

    every_kv = lax.all_gather(key_values, "ctx", axis=1, tiled=True)
    total_rows = every_kv.shape[1]
    chunk = min(2048, total_rows)
    key_pos = mirrored_position(jnp.arange(total_rows, dtype=jnp.int32), count_ctx, tok_ctx)
    key_doc, unused_rope = document_info(key_pos, lengths)
    q_rows = jnp.transpose(queries, (1, 0, 2)).reshape(q_dev * tok_ctx, HEAD_SIZE)
    context = attention_context(
        q_rows,
        every_kv,
        jnp.tile(query_pos, q_dev)[:, None],
        jnp.tile(query_doc, q_dev)[:, None],
        key_pos[None, :],
        key_doc[None, :],
        score_scale,
        chunk,
        q_dev,
    )
    def block_start(block_no):
        holder = jnp.where(block_no < count_ctx, block_no, 2 * count_ctx - 1 - block_no)
        return holder * tok_ctx + jnp.where(block_no < count_ctx, 0, half_rows)

    first_part = lax.dynamic_slice(
        every_kv, (0, block_start(2 * my_ctx), col_offset), (2, half_rows, column_share)
    )
    second_part = lax.dynamic_slice(
        every_kv, (0, block_start(2 * my_ctx + 1), col_offset), (2, half_rows, column_share)
    )
    cache = jnp.concatenate([first_part, second_part], axis=1)
    attn_part = lax.dot_general(
        context, o_turned, (((1,), (1,)), ((), ())), preferred_element_type=jnp.float32
    )
    attn_pieces = lax.all_to_all(
        attn_part.astype(jnp.bfloat16).reshape(expert_count, tok_dev, MODEL_WIDTH),
        "exp",
        split_axis=0,
        concat_axis=0,
        tiled=True,
    )
    attn_pieces, partner_in_low, partner_in_high = lax.optimization_barrier(
        (
            attn_pieces,
            lax.ppermute(expert_in[:, :rows_half], "exp", pair),
            lax.ppermute(expert_in[:, rows_half:], "exp", pair),
        )
    )
    attn_own = jnp.sum(attn_pieces, axis=0, dtype=jnp.float32)
    residual_mid = hidden.astype(jnp.float32) + attn_own
    moe_in = rms_scale(residual_mid, moe_gain).astype(jnp.bfloat16)
    devices = count_ctx * expert_count
    slices = max(1, devices // EXPERTS)
    rows_dev = expert_in.shape[0]
    ffs_dev = expert_out.shape[1]
    capacity = max(4, 2 * tok_dev * TOP // EXPERTS)
    route_ids = routes.reshape(-1)
    route_count = route_ids.shape[0]
    expert_hot = (route_ids[:, None] == jnp.arange(EXPERTS, dtype=jnp.int32)[None, :]).astype(
        jnp.int32
    )
    ranking = jnp.sum(jnp.cumsum(expert_hot, axis=0) * expert_hot, axis=1) - 1
    slot_ids = route_ids * capacity + ranking
    slot_hot = (
        slot_ids[:, None] == jnp.arange(EXPERTS * capacity, dtype=jnp.int32)[None, :]
    ).astype(jnp.bfloat16)
    token_hot = (
        (jnp.arange(route_count, dtype=jnp.int32) // TOP)[:, None]
        == jnp.arange(tok_dev, dtype=jnp.int32)[None, :]
    ).astype(jnp.bfloat16)
    placement_map = jnp.einsum(
        "rs,rt->st", slot_hot, token_hot, preferred_element_type=jnp.float32
    ).astype(jnp.bfloat16)
    experts_ctx = EXPERTS // count_ctx
    share = capacity // slices
    outgoing = jnp.einsum(
        "dct,tf->dcf",
        placement_map.reshape(devices, share, tok_dev),
        moe_in,
        preferred_element_type=jnp.float32,
    ).astype(jnp.bfloat16)
    partner_in = jnp.concatenate([partner_in_low, partner_in_high], axis=1)
    expert_in_both = jnp.concatenate([expert_in, partner_in], axis=0)
    expert_out_both = jnp.concatenate([expert_out, partner_out], axis=0)
    arrived = lax.all_to_all(outgoing, ("ctx", "exp"), split_axis=0, concat_axis=0, tiled=True)
    gate_up = jnp.einsum(
        "dcf,sfh->sdch", arrived, expert_in_both, preferred_element_type=jnp.float32
    )
    activated = (jax.nn.silu(gate_up[..., :ffs_dev]) * gate_up[..., ffs_dev:]).astype(jnp.bfloat16)
    produced = jnp.einsum(
        "sdch,shf->sdcf", activated, expert_out_both, preferred_element_type=jnp.float32
    ).astype(jnp.bfloat16)
    produced = jnp.sum(produced, axis=0, dtype=jnp.float32).astype(jnp.bfloat16)
    returned = lax.all_to_all(produced, ("ctx", "exp"), split_axis=0, concat_axis=0, tiled=True)
    gate_hot = slot_hot.astype(jnp.float32) * gates.reshape(-1)[:, None]
    combiner = jnp.einsum(
        "rs,rt->ts", gate_hot, token_hot.astype(jnp.float32), precision=lax.Precision.HIGHEST
    )
    moe_out = jnp.einsum(
        "tdc,dcf->tf",
        combiner.reshape(tok_dev, devices, share),
        returned.astype(jnp.float32),
        precision=lax.Precision.HIGHEST,
    )
    new_hidden = (residual_mid + moe_out).astype(jnp.bfloat16)
    return (new_hidden, cache)


def solution(mesh):
    in_specs = (
        P(("ctx", "exp"), None),
        P(),
        P(("ctx", "exp"), None),
        P(("ctx", "exp"), None),
        P(),
        P("ctx", "exp"),
        P("ctx", None),
        P(),
        P(),
        P("exp", "ctx"),
        P(),
        P(("ctx", "exp"), None, None),
        P(("ctx", "exp"), None, None),
    )
    out_specs = (P(("ctx", "exp"), None), P(None, "ctx", "exp"))
    return jax.shard_map(shards, mesh=mesh, in_specs=in_specs, out_specs=out_specs, check_vma=False)
```

```python
import jax
import jax.numpy as jnp
from jax import lax
from jax.sharding import PartitionSpec as P
from jax.experimental import pallas as pl
from jax.experimental.pallas import tpu as pltpu

MODEL_WIDTH = 2048
QUERY_HEADS = 32
KEY_VALUE_HEADS = 4
HEAD_SIZE = 128
EXPERTS = 128
TOP = 8


epsilon = 1e-06
rope_base = 1000000.0


def from_behind(block, axis, distance):
    devices = range(lax.axis_size(axis))
    route = [((i - distance) % len(devices), i) for i in devices]
    return lax.ppermute(block, axis, route)


def rms_scale(values, gain):
    mean_square = jnp.mean(values * values, axis=-1, keepdims=True)
    return values * lax.rsqrt(mean_square + epsilon) * gain


def mirrored_position(row_ids, count_ctx, tok_ctx):
    half_rows = tok_ctx // 2
    holder = row_ids // tok_ctx
    within = row_ids % tok_ctx
    block_no = jnp.where(within < half_rows, holder, 2 * count_ctx - 1 - holder)
    return block_no * half_rows + within % half_rows


def document_info(token_positions, lengths):
    first_end = lengths[0]
    second_end = lengths[0] + lengths[1]
    document = (token_positions >= first_end).astype(jnp.int32) + (
        token_positions >= second_end
    ).astype(jnp.int32)
    doc_start = jnp.where(document == 0, 0, jnp.where(document == 1, first_end, second_end))
    return (document, token_positions - doc_start)


def rotate(values, rope_pos):
    head_width = values.shape[-1]
    freq_ids = jnp.arange(head_width // 2, dtype=jnp.float32)
    inverse = rope_base ** (-2.0 * freq_ids / head_width)
    angles = rope_pos.astype(jnp.float32)[:, None] * inverse[None, :]
    cosine = jnp.cos(angles)[:, None, :]
    sine_part = jnp.sin(angles)[:, None, :]
    first_half = values[..., : head_width // 2]
    second_half = values[..., head_width // 2 :]
    return jnp.concatenate(
        [
            first_half * cosine - second_half * sine_part,
            second_half * cosine + first_half * sine_part,
        ],
        axis=-1,
    )


def attention_context(q_rows, every_kv, q_pos, q_doc, k_pos, k_doc, scale, chunk, heads):
    rows, width = q_rows.shape
    tok = rows // heads
    total = every_kv.shape[1]
    steps = total // chunk

    def body(q_ref, k_ref, v_ref, qp_ref, qd_ref, kp_ref, kd_ref, out_ref, num_acc, den_acc):
        step = pl.program_id(0)

        @pl.when(step == 0)
        def _():
            num_acc[...] = jnp.zeros_like(num_acc)
            den_acc[...] = jnp.zeros_like(den_acc)

        scores = (
            lax.dot_general(
                q_ref[...], k_ref[...], (((1,), (1,)), ((), ())),
                preferred_element_type=jnp.float32,
            )
            * scale
        )
        allowed = (qd_ref[...] == kd_ref[...]) & (kp_ref[...] <= qp_ref[...])
        weights = jnp.where(allowed, jnp.exp(scores), 0.0).astype(jnp.bfloat16)
        values = v_ref[...]
        values_one = jnp.concatenate([values, jnp.ones_like(values)], axis=1)
        both = jnp.dot(weights, values_one, preferred_element_type=jnp.float32)
        num_acc[...] += both[:, :width]
        den_acc[...] += both[:, width : width + 1]

        @pl.when(step == steps - 1)
        def _():
            for head in range(heads):
                part = slice(head * tok, (head + 1) * tok)
                out_ref[:, head * width : (head + 1) * width] = (
                    num_acc[part, :] / den_acc[part, :]
                ).astype(out_ref.dtype)

    whole = lambda i: (0, 0)
    return pl.pallas_call(
        body,
        grid=(steps,),
        in_specs=[
            pl.BlockSpec((rows, width), whole),
            pl.BlockSpec((None, chunk, width), lambda i: (0, i, 0)),
            pl.BlockSpec((None, chunk, width), lambda i: (1, i, 0)),
            pl.BlockSpec((rows, 1), whole),
            pl.BlockSpec((rows, 1), whole),
            pl.BlockSpec((1, chunk), lambda i: (0, i)),
            pl.BlockSpec((1, chunk), lambda i: (0, i)),
        ],
        out_specs=pl.BlockSpec((tok, heads * width), whole),
        out_shape=jax.ShapeDtypeStruct((tok, heads * width), jnp.bfloat16),
        scratch_shapes=[pltpu.VMEM((rows, width), jnp.float32), pltpu.VMEM((rows, 1), jnp.float32)],
        compiler_params=pltpu.CompilerParams(dimension_semantics=("arbitrary",)),
    )(q_rows, every_kv, every_kv, q_pos, q_doc, k_pos, k_doc)


def shards(
    hidden,
    lengths,
    routes,
    gates,
    attn_gain,
    q_weight,
    key_value_weight,
    q_gain,
    k_gain,
    o_weight,
    moe_gain,
    expert_in,
    expert_out,
):
    count_ctx = lax.axis_size("ctx")
    expert_count = lax.axis_size("exp")
    my_ctx = lax.axis_index("ctx")
    my_exp = lax.axis_index("exp")
    tok_dev = hidden.shape[0]
    tok_ctx = tok_dev * expert_count
    half_rows = tok_ctx // 2
    head_groups = QUERY_HEADS // KEY_VALUE_HEADS
    q_dev = QUERY_HEADS // expert_count
    key_value_share = max(1, KEY_VALUE_HEADS // expert_count)
    group_dev = q_dev // key_value_share
    column_share = KEY_VALUE_HEADS * HEAD_SIZE // expert_count
    key_value_leading = my_exp * q_dev // head_groups
    col_offset = my_exp * column_share - key_value_leading * HEAD_SIZE
    score_scale = HEAD_SIZE ** (-0.5)
    query_pos = mirrored_position(
        my_ctx * tok_ctx + jnp.arange(tok_ctx, dtype=jnp.int32), count_ctx, tok_ctx
    )
    query_doc, query_rope = document_info(query_pos, lengths)
    normed_own = rms_scale(hidden.astype(jnp.float32), attn_gain).astype(jnp.bfloat16)
    normed = lax.all_to_all(
        jnp.broadcast_to(normed_own[None], (expert_count,) + normed_own.shape),
        "exp",
        split_axis=0,
        concat_axis=0,
        tiled=True,
    ).reshape(tok_ctx, MODEL_WIDTH)
    key_cols = lax.dynamic_slice_in_dim(
        key_value_weight, key_value_leading * HEAD_SIZE, key_value_share * HEAD_SIZE, 1
    )
    value_column_block = lax.dynamic_slice_in_dim(
        key_value_weight,
        KEY_VALUE_HEADS * HEAD_SIZE + key_value_leading * HEAD_SIZE,
        key_value_share * HEAD_SIZE,
        1,
    )
    kv_local = jnp.concatenate([key_cols, value_column_block], axis=1)
    q_width = q_dev * HEAD_SIZE
    pair = [(i, i ^ 1) for i in range(expert_count)]
    rows_half = expert_in.shape[1] // 2
    weights_all, partner_out = lax.optimization_barrier(
        (
            lax.all_gather(
                jnp.concatenate([q_weight, kv_local, o_weight.T], axis=1), "ctx", axis=0, tiled=True
            ),
            lax.ppermute(lax.optimization_barrier((expert_out, normed))[0], "exp", pair),
        )
    )
    kv_width = kv_local.shape[1]
    key_value_plain = jnp.dot(
        normed, weights_all[:, q_width : q_width + kv_width], preferred_element_type=jnp.float32
    )
    q_raw = jnp.dot(normed, weights_all[:, :q_width], preferred_element_type=jnp.float32)
    o_turned = weights_all[:, q_width + kv_width :]
    queries = rotate(
        rms_scale(q_raw.reshape(tok_ctx, q_dev, HEAD_SIZE), q_gain), query_rope
    ).astype(jnp.bfloat16)
    key_row_block = rotate(
        rms_scale(
            key_value_plain[:, : key_value_share * HEAD_SIZE].reshape(
                tok_ctx, key_value_share, HEAD_SIZE
            ),
            k_gain,
        ),
        query_rope,
    ).astype(jnp.bfloat16)
    value_row_block = key_value_plain[:, key_value_share * HEAD_SIZE :].astype(jnp.bfloat16)
    key_values = jnp.stack(
        [key_row_block.reshape(tok_ctx, key_value_share * HEAD_SIZE), value_row_block]
    )

    every_kv = lax.all_gather(key_values, "ctx", axis=1, tiled=True)
    total_rows = every_kv.shape[1]
    chunk = min(1024, total_rows)
    key_pos = mirrored_position(jnp.arange(total_rows, dtype=jnp.int32), count_ctx, tok_ctx)
    key_doc, unused_rope = document_info(key_pos, lengths)
    q_rows = jnp.transpose(queries, (1, 0, 2)).reshape(q_dev * tok_ctx, HEAD_SIZE)
    context = attention_context(
        q_rows,
        every_kv,
        jnp.tile(query_pos, q_dev)[:, None],
        jnp.tile(query_doc, q_dev)[:, None],
        key_pos[None, :],
        key_doc[None, :],
        score_scale,
        chunk,
        q_dev,
    )
    def block_start(block_no):
        holder = jnp.where(block_no < count_ctx, block_no, 2 * count_ctx - 1 - block_no)
        return holder * tok_ctx + jnp.where(block_no < count_ctx, 0, half_rows)

    first_part = lax.dynamic_slice(
        every_kv, (0, block_start(2 * my_ctx), col_offset), (2, half_rows, column_share)
    )
    second_part = lax.dynamic_slice(
        every_kv, (0, block_start(2 * my_ctx + 1), col_offset), (2, half_rows, column_share)
    )
    cache = jnp.concatenate([first_part, second_part], axis=1)
    attn_part = lax.dot_general(
        context, o_turned, (((1,), (1,)), ((), ())), preferred_element_type=jnp.float32
    )
    attn_pieces = lax.all_to_all(
        attn_part.astype(jnp.bfloat16).reshape(expert_count, tok_dev, MODEL_WIDTH),
        "exp",
        split_axis=0,
        concat_axis=0,
        tiled=True,
    )
    attn_pieces, partner_in_low, partner_in_high = lax.optimization_barrier(
        (
            attn_pieces,
            lax.ppermute(expert_in[:, :rows_half], "exp", pair),
            lax.ppermute(expert_in[:, rows_half:], "exp", pair),
        )
    )
    attn_own = jnp.sum(attn_pieces, axis=0, dtype=jnp.float32)
    residual_mid = hidden.astype(jnp.float32) + attn_own
    moe_in = rms_scale(residual_mid, moe_gain).astype(jnp.bfloat16)
    devices = count_ctx * expert_count
    slices = max(1, devices // EXPERTS)
    rows_dev = expert_in.shape[0]
    ffs_dev = expert_out.shape[1]
    capacity = max(4, 2 * tok_dev * TOP // EXPERTS)
    route_ids = routes.reshape(-1)
    route_count = route_ids.shape[0]
    expert_hot = (route_ids[:, None] == jnp.arange(EXPERTS, dtype=jnp.int32)[None, :]).astype(
        jnp.int32
    )
    ranking = jnp.sum(jnp.cumsum(expert_hot, axis=0) * expert_hot, axis=1) - 1
    slot_ids = route_ids * capacity + ranking
    slot_hot = (
        slot_ids[:, None] == jnp.arange(EXPERTS * capacity, dtype=jnp.int32)[None, :]
    ).astype(jnp.bfloat16)
    token_hot = (
        (jnp.arange(route_count, dtype=jnp.int32) // TOP)[:, None]
        == jnp.arange(tok_dev, dtype=jnp.int32)[None, :]
    ).astype(jnp.bfloat16)
    placement_map = jnp.einsum(
        "rs,rt->st", slot_hot, token_hot, preferred_element_type=jnp.float32
    ).astype(jnp.bfloat16)
    experts_ctx = EXPERTS // count_ctx
    share = capacity // slices
    outgoing = jnp.einsum(
        "dct,tf->dcf",
        placement_map.reshape(devices, share, tok_dev),
        moe_in,
        preferred_element_type=jnp.float32,
    ).astype(jnp.bfloat16)
    partner_in = jnp.concatenate([partner_in_low, partner_in_high], axis=1)
    expert_in_both = jnp.concatenate([expert_in, partner_in], axis=0)
    expert_out_both = jnp.concatenate([expert_out, partner_out], axis=0)
    arrived = lax.all_to_all(outgoing, ("ctx", "exp"), split_axis=0, concat_axis=0, tiled=True)
    gate_up = jnp.einsum(
        "dcf,sfh->sdch", arrived, expert_in_both, preferred_element_type=jnp.float32
    )
    activated = (jax.nn.silu(gate_up[..., :ffs_dev]) * gate_up[..., ffs_dev:]).astype(jnp.bfloat16)
    produced = jnp.einsum(
        "sdch,shf->sdcf", activated, expert_out_both, preferred_element_type=jnp.float32
    ).astype(jnp.bfloat16)
    produced = jnp.sum(produced, axis=0, dtype=jnp.float32).astype(jnp.bfloat16)
    returned = lax.all_to_all(produced, ("ctx", "exp"), split_axis=0, concat_axis=0, tiled=True)
    gate_hot = slot_hot.astype(jnp.float32) * gates.reshape(-1)[:, None]
    combiner = jnp.einsum(
        "rs,rt->ts", gate_hot, token_hot.astype(jnp.float32), precision=lax.Precision.HIGHEST
    )
    moe_out = jnp.einsum(
        "tdc,dcf->tf",
        combiner.reshape(tok_dev, devices, share),
        returned.astype(jnp.float32),
        precision=lax.Precision.HIGHEST,
    )
    new_hidden = (residual_mid + moe_out).astype(jnp.bfloat16)
    return (new_hidden, cache)


def solution(mesh):
    in_specs = (
        P(("ctx", "exp"), None),
        P(),
        P(("ctx", "exp"), None),
        P(("ctx", "exp"), None),
        P(),
        P("ctx", "exp"),
        P("ctx", None),
        P(),
        P(),
        P("exp", "ctx"),
        P(),
        P(("ctx", "exp"), None, None),
        P(("ctx", "exp"), None, None),
    )
    out_specs = (P(("ctx", "exp"), None), P(None, "ctx", "exp"))
    return jax.shard_map(shards, mesh=mesh, in_specs=in_specs, out_specs=out_specs, check_vma=False)
```

```python
import jax
import jax.numpy as jnp
from jax import lax
from jax.sharding import PartitionSpec as P
from jax.experimental import pallas as pl
from jax.experimental.pallas import tpu as pltpu

MODEL_WIDTH = 2048
QUERY_HEADS = 32
KEY_VALUE_HEADS = 4
HEAD_SIZE = 128
EXPERTS = 128
TOP = 8


epsilon = 1e-06
rope_base = 1000000.0


def from_behind(block, axis, distance):
    devices = range(lax.axis_size(axis))
    route = [((i - distance) % len(devices), i) for i in devices]
    return lax.ppermute(block, axis, route)


def rms_scale(values, gain):
    mean_square = jnp.mean(values * values, axis=-1, keepdims=True)
    return values * lax.rsqrt(mean_square + epsilon) * gain


def mirrored_position(row_ids, count_ctx, tok_ctx):
    half_rows = tok_ctx // 2
    holder = row_ids // tok_ctx
    within = row_ids % tok_ctx
    block_no = jnp.where(within < half_rows, holder, 2 * count_ctx - 1 - holder)
    return block_no * half_rows + within % half_rows


def document_info(token_positions, lengths):
    first_end = lengths[0]
    second_end = lengths[0] + lengths[1]
    document = (token_positions >= first_end).astype(jnp.int32) + (
        token_positions >= second_end
    ).astype(jnp.int32)
    doc_start = jnp.where(document == 0, 0, jnp.where(document == 1, first_end, second_end))
    return (document, token_positions - doc_start)


def rotate(values, rope_pos):
    head_width = values.shape[-1]
    freq_ids = jnp.arange(head_width // 2, dtype=jnp.float32)
    inverse = rope_base ** (-2.0 * freq_ids / head_width)
    angles = rope_pos.astype(jnp.float32)[:, None] * inverse[None, :]
    cosine = jnp.cos(angles)[:, None, :]
    sine_part = jnp.sin(angles)[:, None, :]
    first_half = values[..., : head_width // 2]
    second_half = values[..., head_width // 2 :]
    return jnp.concatenate(
        [
            first_half * cosine - second_half * sine_part,
            second_half * cosine + first_half * sine_part,
        ],
        axis=-1,
    )


def attention_context(q_rows, every_kv, q_pos, q_doc, k_pos, k_doc, scale, chunk, heads):
    rows, width = q_rows.shape
    tok = rows // heads
    total = every_kv.shape[1]
    steps = total // chunk

    def body(q_ref, k_ref, v_ref, qp_ref, qd_ref, kp_ref, kd_ref, out_ref, num_acc, den_acc):
        step = pl.program_id(0)

        @pl.when(step == 0)
        def _():
            num_acc[...] = jnp.zeros_like(num_acc)
            den_acc[...] = jnp.zeros_like(den_acc)

        scores = (
            lax.dot_general(
                q_ref[...], k_ref[...], (((1,), (1,)), ((), ())),
                preferred_element_type=jnp.float32,
            )
            * scale
        )
        allowed = (qd_ref[...] == kd_ref[...]) & (kp_ref[...] <= qp_ref[...])
        weights = jnp.where(allowed, jnp.exp(scores), 0.0).astype(jnp.bfloat16)
        values = v_ref[...]
        values_one = jnp.concatenate([values, jnp.ones_like(values)], axis=1)
        both = jnp.dot(weights, values_one, preferred_element_type=jnp.float32)
        num_acc[...] += both[:, :width]
        den_acc[...] += both[:, width : width + 1]

        @pl.when(step == steps - 1)
        def _():
            for head in range(heads):
                part = slice(head * tok, (head + 1) * tok)
                out_ref[:, head * width : (head + 1) * width] = (
                    num_acc[part, :] / den_acc[part, :]
                ).astype(out_ref.dtype)

    whole = lambda i: (0, 0)
    return pl.pallas_call(
        body,
        grid=(steps,),
        in_specs=[
            pl.BlockSpec((rows, width), whole),
            pl.BlockSpec((None, chunk, width), lambda i: (0, i, 0)),
            pl.BlockSpec((None, chunk, width), lambda i: (1, i, 0)),
            pl.BlockSpec((rows, 1), whole),
            pl.BlockSpec((rows, 1), whole),
            pl.BlockSpec((1, chunk), lambda i: (0, i)),
            pl.BlockSpec((1, chunk), lambda i: (0, i)),
        ],
        out_specs=pl.BlockSpec((tok, heads * width), whole),
        out_shape=jax.ShapeDtypeStruct((tok, heads * width), jnp.bfloat16),
        scratch_shapes=[pltpu.VMEM((rows, width), jnp.float32), pltpu.VMEM((rows, 1), jnp.float32)],
        compiler_params=pltpu.CompilerParams(dimension_semantics=("arbitrary",)),
    )(q_rows, every_kv, every_kv, q_pos, q_doc, k_pos, k_doc)


def shards(
    hidden,
    lengths,
    routes,
    gates,
    attn_gain,
    q_weight,
    key_value_weight,
    q_gain,
    k_gain,
    o_weight,
    moe_gain,
    expert_in,
    expert_out,
):
    count_ctx = lax.axis_size("ctx")
    expert_count = lax.axis_size("exp")
    my_ctx = lax.axis_index("ctx")
    my_exp = lax.axis_index("exp")
    tok_dev = hidden.shape[0]
    tok_ctx = tok_dev * expert_count
    half_rows = tok_ctx // 2
    head_groups = QUERY_HEADS // KEY_VALUE_HEADS
    q_dev = QUERY_HEADS // expert_count
    key_value_share = max(1, KEY_VALUE_HEADS // expert_count)
    group_dev = q_dev // key_value_share
    column_share = KEY_VALUE_HEADS * HEAD_SIZE // expert_count
    key_value_leading = my_exp * q_dev // head_groups
    col_offset = my_exp * column_share - key_value_leading * HEAD_SIZE
    score_scale = HEAD_SIZE ** (-0.5)
    query_pos = mirrored_position(
        my_ctx * tok_ctx + jnp.arange(tok_ctx, dtype=jnp.int32), count_ctx, tok_ctx
    )
    query_doc, query_rope = document_info(query_pos, lengths)
    normed_own = rms_scale(hidden.astype(jnp.float32), attn_gain).astype(jnp.bfloat16)
    normed = lax.all_to_all(
        jnp.broadcast_to(normed_own[None], (expert_count,) + normed_own.shape),
        "exp",
        split_axis=0,
        concat_axis=0,
        tiled=True,
    ).reshape(tok_ctx, MODEL_WIDTH)
    key_cols = lax.dynamic_slice_in_dim(
        key_value_weight, key_value_leading * HEAD_SIZE, key_value_share * HEAD_SIZE, 1
    )
    value_column_block = lax.dynamic_slice_in_dim(
        key_value_weight,
        KEY_VALUE_HEADS * HEAD_SIZE + key_value_leading * HEAD_SIZE,
        key_value_share * HEAD_SIZE,
        1,
    )
    kv_local = jnp.concatenate([key_cols, value_column_block], axis=1)
    q_width = q_dev * HEAD_SIZE
    pair = [(i, i ^ 1) for i in range(expert_count)]
    rows_half = expert_in.shape[1] // 2
    weights_all, partner_out = lax.optimization_barrier(
        (
            lax.all_gather(
                jnp.concatenate([q_weight, kv_local, o_weight.T], axis=1), "ctx", axis=0, tiled=True
            ),
            lax.ppermute(expert_out, "exp", pair),
        )
    )
    kv_width = kv_local.shape[1]
    key_value_plain = jnp.dot(
        normed, weights_all[:, q_width : q_width + kv_width], preferred_element_type=jnp.float32
    )
    q_raw = jnp.dot(normed, weights_all[:, :q_width], preferred_element_type=jnp.float32)
    o_turned = weights_all[:, q_width + kv_width :]
    queries = rotate(
        rms_scale(q_raw.reshape(tok_ctx, q_dev, HEAD_SIZE), q_gain), query_rope
    ).astype(jnp.bfloat16)
    key_row_block = rotate(
        rms_scale(
            key_value_plain[:, : key_value_share * HEAD_SIZE].reshape(
                tok_ctx, key_value_share, HEAD_SIZE
            ),
            k_gain,
        ),
        query_rope,
    ).astype(jnp.bfloat16)
    value_row_block = key_value_plain[:, key_value_share * HEAD_SIZE :].astype(jnp.bfloat16)
    key_values = jnp.stack(
        [key_row_block.reshape(tok_ctx, key_value_share * HEAD_SIZE), value_row_block]
    )

    every_kv = lax.all_gather(key_values, "ctx", axis=1, tiled=True)
    total_rows = every_kv.shape[1]
    chunk = min(1024, total_rows)
    key_pos = mirrored_position(jnp.arange(total_rows, dtype=jnp.int32), count_ctx, tok_ctx)
    key_doc, unused_rope = document_info(key_pos, lengths)
    q_rows = jnp.transpose(queries, (1, 0, 2)).reshape(q_dev * tok_ctx, HEAD_SIZE)
    context = attention_context(
        q_rows,
        every_kv,
        jnp.tile(query_pos, q_dev)[:, None],
        jnp.tile(query_doc, q_dev)[:, None],
        key_pos[None, :],
        key_doc[None, :],
        score_scale,
        chunk,
        q_dev,
    )
    def block_start(block_no):
        holder = jnp.where(block_no < count_ctx, block_no, 2 * count_ctx - 1 - block_no)
        return holder * tok_ctx + jnp.where(block_no < count_ctx, 0, half_rows)

    first_part = lax.dynamic_slice(
        every_kv, (0, block_start(2 * my_ctx), col_offset), (2, half_rows, column_share)
    )
    second_part = lax.dynamic_slice(
        every_kv, (0, block_start(2 * my_ctx + 1), col_offset), (2, half_rows, column_share)
    )
    cache = jnp.concatenate([first_part, second_part], axis=1)
    attn_part = lax.dot_general(
        context, o_turned, (((1,), (1,)), ((), ())), preferred_element_type=jnp.float32
    )
    attn_pieces = lax.all_to_all(
        attn_part.astype(jnp.bfloat16).reshape(expert_count, tok_dev, MODEL_WIDTH),
        "exp",
        split_axis=0,
        concat_axis=0,
        tiled=True,
    )
    attn_pieces, partner_in_low, partner_in_high = lax.optimization_barrier(
        (
            attn_pieces,
            lax.ppermute(expert_in[:, :rows_half], "exp", pair),
            lax.ppermute(expert_in[:, rows_half:], "exp", pair),
        )
    )
    attn_own = jnp.sum(attn_pieces, axis=0, dtype=jnp.float32)
    residual_mid = hidden.astype(jnp.float32) + attn_own
    moe_in = rms_scale(residual_mid, moe_gain).astype(jnp.bfloat16)
    devices = count_ctx * expert_count
    slices = max(1, devices // EXPERTS)
    rows_dev = expert_in.shape[0]
    ffs_dev = expert_out.shape[1]
    capacity = max(4, 2 * tok_dev * TOP // EXPERTS)
    route_ids = routes.reshape(-1)
    route_count = route_ids.shape[0]
    expert_hot = (route_ids[:, None] == jnp.arange(EXPERTS, dtype=jnp.int32)[None, :]).astype(
        jnp.int32
    )
    ranking = jnp.sum(jnp.cumsum(expert_hot, axis=0) * expert_hot, axis=1) - 1
    slot_ids = route_ids * capacity + ranking
    slot_hot = (
        slot_ids[:, None] == jnp.arange(EXPERTS * capacity, dtype=jnp.int32)[None, :]
    ).astype(jnp.bfloat16)
    token_hot = (
        (jnp.arange(route_count, dtype=jnp.int32) // TOP)[:, None]
        == jnp.arange(tok_dev, dtype=jnp.int32)[None, :]
    ).astype(jnp.bfloat16)
    placement_map = jnp.einsum(
        "rs,rt->st", slot_hot, token_hot, preferred_element_type=jnp.float32
    ).astype(jnp.bfloat16)
    experts_ctx = EXPERTS // count_ctx
    share = capacity // slices
    outgoing = jnp.einsum(
        "dct,tf->dcf",
        placement_map.reshape(devices, share, tok_dev),
        moe_in,
        preferred_element_type=jnp.float32,
    ).astype(jnp.bfloat16)
    partner_in = jnp.concatenate([partner_in_low, partner_in_high], axis=1)
    expert_in_both = jnp.concatenate([expert_in, partner_in], axis=0)
    expert_out_both = jnp.concatenate([expert_out, partner_out], axis=0)
    arrived = lax.all_to_all(outgoing, ("ctx", "exp"), split_axis=0, concat_axis=0, tiled=True)
    gate_up = jnp.einsum(
        "dcf,sfh->sdch", arrived, expert_in_both, preferred_element_type=jnp.float32
    )
    activated = (jax.nn.silu(gate_up[..., :ffs_dev]) * gate_up[..., ffs_dev:]).astype(jnp.bfloat16)
    produced = jnp.einsum(
        "sdch,shf->sdcf", activated, expert_out_both, preferred_element_type=jnp.float32
    ).astype(jnp.bfloat16)
    produced = jnp.sum(produced, axis=0, dtype=jnp.float32).astype(jnp.bfloat16)
    returned = lax.all_to_all(produced, ("ctx", "exp"), split_axis=0, concat_axis=0, tiled=True)
    gate_hot = slot_hot.astype(jnp.float32) * gates.reshape(-1)[:, None]
    combiner = jnp.einsum(
        "rs,rt->ts", gate_hot, token_hot.astype(jnp.float32), precision=lax.Precision.HIGHEST
    )
    moe_out = jnp.einsum(
        "tdc,dcf->tf",
        combiner.reshape(tok_dev, devices, share),
        returned.astype(jnp.float32),
        precision=lax.Precision.HIGHEST,
    )
    new_hidden = (residual_mid + moe_out).astype(jnp.bfloat16)
    return (new_hidden, cache)


def solution(mesh):
    in_specs = (
        P(("ctx", "exp"), None),
        P(),
        P(("ctx", "exp"), None),
        P(("ctx", "exp"), None),
        P(),
        P("ctx", "exp"),
        P("ctx", None),
        P(),
        P(),
        P("exp", "ctx"),
        P(),
        P(("ctx", "exp"), None, None),
        P(("ctx", "exp"), None, None),
    )
    out_specs = (P(("ctx", "exp"), None), P(None, "ctx", "exp"))
    return jax.shard_map(shards, mesh=mesh, in_specs=in_specs, out_specs=out_specs, check_vma=False)
```

```python
import jax
import jax.numpy as jnp
from jax import lax
from jax.sharding import PartitionSpec as P
from jax.experimental import pallas as pl
from jax.experimental.pallas import tpu as pltpu

MODEL_WIDTH = 2048
QUERY_HEADS = 32
KEY_VALUE_HEADS = 4
HEAD_SIZE = 128
EXPERTS = 128
TOP = 8


epsilon = 1e-06
rope_base = 1000000.0


def from_behind(block, axis, distance):
    devices = range(lax.axis_size(axis))
    route = [((i - distance) % len(devices), i) for i in devices]
    return lax.ppermute(block, axis, route)


def rms_scale(values, gain):
    mean_square = jnp.mean(values * values, axis=-1, keepdims=True)
    return values * lax.rsqrt(mean_square + epsilon) * gain


def mirrored_position(row_ids, count_ctx, tok_ctx):
    half_rows = tok_ctx // 2
    holder = row_ids // tok_ctx
    within = row_ids % tok_ctx
    block_no = jnp.where(within < half_rows, holder, 2 * count_ctx - 1 - holder)
    return block_no * half_rows + within % half_rows


def document_info(token_positions, lengths):
    first_end = lengths[0]
    second_end = lengths[0] + lengths[1]
    document = (token_positions >= first_end).astype(jnp.int32) + (
        token_positions >= second_end
    ).astype(jnp.int32)
    doc_start = jnp.where(document == 0, 0, jnp.where(document == 1, first_end, second_end))
    return (document, token_positions - doc_start)


def rotate(values, rope_pos):
    head_width = values.shape[-1]
    freq_ids = jnp.arange(head_width // 2, dtype=jnp.float32)
    inverse = rope_base ** (-2.0 * freq_ids / head_width)
    angles = rope_pos.astype(jnp.float32)[:, None] * inverse[None, :]
    cosine = jnp.cos(angles)[:, None, :]
    sine_part = jnp.sin(angles)[:, None, :]
    first_half = values[..., : head_width // 2]
    second_half = values[..., head_width // 2 :]
    return jnp.concatenate(
        [
            first_half * cosine - second_half * sine_part,
            second_half * cosine + first_half * sine_part,
        ],
        axis=-1,
    )


def attention_context(q_rows, every_kv, q_pos, q_doc, k_pos, k_doc, scale, chunk, heads):
    rows, width = q_rows.shape
    tok = rows // heads
    total = every_kv.shape[1]
    steps = total // chunk

    def body(q_ref, k_ref, v_ref, qp_ref, qd_ref, kp_ref, kd_ref, out_ref, num_acc, den_acc):
        step = pl.program_id(0)

        @pl.when(step == 0)
        def _():
            num_acc[...] = jnp.zeros_like(num_acc)
            den_acc[...] = jnp.zeros_like(den_acc)

        scores = (
            lax.dot_general(
                q_ref[...], k_ref[...], (((1,), (1,)), ((), ())),
                preferred_element_type=jnp.float32,
            )
            * scale
        )
        start = qd_ref[...]
        allowed = (kp_ref[...] - start).astype(jnp.uint32) <= (qp_ref[...] - start).astype(jnp.uint32)
        weights = jnp.where(allowed, jnp.exp(scores), 0.0).astype(jnp.bfloat16)
        values = v_ref[...]
        values_one = jnp.concatenate([values, jnp.ones_like(values)], axis=1)
        both = jnp.dot(weights, values_one, preferred_element_type=jnp.float32)
        num_acc[...] += both[:, :width]
        den_acc[...] += both[:, width : width + 1]

        @pl.when(step == steps - 1)
        def _():
            for head in range(heads):
                part = slice(head * tok, (head + 1) * tok)
                out_ref[:, head * width : (head + 1) * width] = (
                    num_acc[part, :] / den_acc[part, :]
                ).astype(out_ref.dtype)

    whole = lambda i: (0, 0)
    return pl.pallas_call(
        body,
        grid=(steps,),
        in_specs=[
            pl.BlockSpec((rows, width), whole),
            pl.BlockSpec((None, chunk, width), lambda i: (0, i, 0)),
            pl.BlockSpec((None, chunk, width), lambda i: (1, i, 0)),
            pl.BlockSpec((rows, 1), whole),
            pl.BlockSpec((rows, 1), whole),
            pl.BlockSpec((1, chunk), lambda i: (0, i)),
            pl.BlockSpec((1, chunk), lambda i: (0, i)),
        ],
        out_specs=pl.BlockSpec((tok, heads * width), whole),
        out_shape=jax.ShapeDtypeStruct((tok, heads * width), jnp.bfloat16),
        scratch_shapes=[pltpu.VMEM((rows, width), jnp.float32), pltpu.VMEM((rows, 1), jnp.float32)],
        compiler_params=pltpu.CompilerParams(dimension_semantics=("arbitrary",)),
    )(q_rows, every_kv, every_kv, q_pos, q_doc, k_pos, k_doc)


def shards(
    hidden,
    lengths,
    routes,
    gates,
    attn_gain,
    q_weight,
    key_value_weight,
    q_gain,
    k_gain,
    o_weight,
    moe_gain,
    expert_in,
    expert_out,
):
    count_ctx = lax.axis_size("ctx")
    expert_count = lax.axis_size("exp")
    my_ctx = lax.axis_index("ctx")
    my_exp = lax.axis_index("exp")
    tok_dev = hidden.shape[0]
    tok_ctx = tok_dev * expert_count
    half_rows = tok_ctx // 2
    head_groups = QUERY_HEADS // KEY_VALUE_HEADS
    q_dev = QUERY_HEADS // expert_count
    key_value_share = max(1, KEY_VALUE_HEADS // expert_count)
    group_dev = q_dev // key_value_share
    column_share = KEY_VALUE_HEADS * HEAD_SIZE // expert_count
    key_value_leading = my_exp * q_dev // head_groups
    col_offset = my_exp * column_share - key_value_leading * HEAD_SIZE
    score_scale = HEAD_SIZE ** (-0.5)
    query_pos = mirrored_position(
        my_ctx * tok_ctx + jnp.arange(tok_ctx, dtype=jnp.int32), count_ctx, tok_ctx
    )
    query_doc, query_rope = document_info(query_pos, lengths)
    normed_own = rms_scale(hidden.astype(jnp.float32), attn_gain).astype(jnp.bfloat16)
    normed = lax.all_to_all(
        jnp.broadcast_to(normed_own[None], (expert_count,) + normed_own.shape),
        "exp",
        split_axis=0,
        concat_axis=0,
        tiled=True,
    ).reshape(tok_ctx, MODEL_WIDTH)
    key_cols = lax.dynamic_slice_in_dim(
        key_value_weight, key_value_leading * HEAD_SIZE, key_value_share * HEAD_SIZE, 1
    )
    value_column_block = lax.dynamic_slice_in_dim(
        key_value_weight,
        KEY_VALUE_HEADS * HEAD_SIZE + key_value_leading * HEAD_SIZE,
        key_value_share * HEAD_SIZE,
        1,
    )
    kv_local = jnp.concatenate([key_cols, value_column_block], axis=1)
    q_width = q_dev * HEAD_SIZE
    pair = [(i, i ^ 1) for i in range(expert_count)]
    rows_half = expert_in.shape[1] // 2
    weights_all, partner_out = lax.optimization_barrier(
        (
            lax.all_gather(
                jnp.concatenate([q_weight, kv_local, o_weight.T], axis=1), "ctx", axis=0, tiled=True
            ),
            lax.ppermute(expert_out, "exp", pair),
        )
    )
    kv_width = kv_local.shape[1]
    projected = jnp.dot(
        normed, weights_all[:, : q_width + kv_width], preferred_element_type=jnp.float32
    )
    o_turned = weights_all[:, q_width + kv_width :]
    q_raw = projected[:, :q_width]
    key_value_plain = projected[:, q_width:]
    queries = rotate(
        rms_scale(q_raw.reshape(tok_ctx, q_dev, HEAD_SIZE), q_gain), query_rope
    ).astype(jnp.bfloat16)
    key_row_block = rotate(
        rms_scale(
            key_value_plain[:, : key_value_share * HEAD_SIZE].reshape(
                tok_ctx, key_value_share, HEAD_SIZE
            ),
            k_gain,
        ),
        query_rope,
    ).astype(jnp.bfloat16)
    value_row_block = key_value_plain[:, key_value_share * HEAD_SIZE :].astype(jnp.bfloat16)
    key_values = jnp.stack(
        [key_row_block.reshape(tok_ctx, key_value_share * HEAD_SIZE), value_row_block]
    )

    every_kv = lax.all_gather(key_values, "ctx", axis=1, tiled=True)
    total_rows = every_kv.shape[1]
    chunk = min(1024, total_rows)
    key_pos = mirrored_position(jnp.arange(total_rows, dtype=jnp.int32), count_ctx, tok_ctx)
    key_doc, unused_rope = document_info(key_pos, lengths)
    q_rows = jnp.transpose(queries, (1, 0, 2)).reshape(q_dev * tok_ctx, HEAD_SIZE)
    context = attention_context(
        q_rows,
        every_kv,
        jnp.tile(query_pos, q_dev)[:, None],
        jnp.tile(query_pos - query_rope, q_dev)[:, None],
        key_pos[None, :],
        key_doc[None, :],
        score_scale,
        chunk,
        q_dev,
    )
    def block_start(block_no):
        holder = jnp.where(block_no < count_ctx, block_no, 2 * count_ctx - 1 - block_no)
        return holder * tok_ctx + jnp.where(block_no < count_ctx, 0, half_rows)

    first_part = lax.dynamic_slice(
        every_kv, (0, block_start(2 * my_ctx), col_offset), (2, half_rows, column_share)
    )
    second_part = lax.dynamic_slice(
        every_kv, (0, block_start(2 * my_ctx + 1), col_offset), (2, half_rows, column_share)
    )
    cache = jnp.concatenate([first_part, second_part], axis=1)
    attn_part = lax.dot_general(
        context, o_turned, (((1,), (1,)), ((), ())), preferred_element_type=jnp.float32
    )
    attn_pieces = lax.all_to_all(
        attn_part.astype(jnp.bfloat16).reshape(expert_count, tok_dev, MODEL_WIDTH),
        "exp",
        split_axis=0,
        concat_axis=0,
        tiled=True,
    )
    attn_pieces, partner_in_low, partner_in_high = lax.optimization_barrier(
        (
            attn_pieces,
            lax.ppermute(expert_in[:, :rows_half], "exp", pair),
            lax.ppermute(expert_in[:, rows_half:], "exp", pair),
        )
    )
    attn_own = jnp.sum(attn_pieces, axis=0, dtype=jnp.float32)
    residual_mid = hidden.astype(jnp.float32) + attn_own
    moe_in = rms_scale(residual_mid, moe_gain).astype(jnp.bfloat16)
    devices = count_ctx * expert_count
    slices = max(1, devices // EXPERTS)
    rows_dev = expert_in.shape[0]
    ffs_dev = expert_out.shape[1]
    capacity = max(4, 2 * tok_dev * TOP // EXPERTS)
    route_ids = routes.reshape(-1)
    route_count = route_ids.shape[0]
    expert_hot = (route_ids[:, None] == jnp.arange(EXPERTS, dtype=jnp.int32)[None, :]).astype(
        jnp.int32
    )
    ranking = jnp.sum(jnp.cumsum(expert_hot, axis=0) * expert_hot, axis=1) - 1
    slot_ids = route_ids * capacity + ranking
    slot_hot = (
        slot_ids[:, None] == jnp.arange(EXPERTS * capacity, dtype=jnp.int32)[None, :]
    ).astype(jnp.bfloat16)
    token_hot = (
        (jnp.arange(route_count, dtype=jnp.int32) // TOP)[:, None]
        == jnp.arange(tok_dev, dtype=jnp.int32)[None, :]
    ).astype(jnp.bfloat16)
    placement_map = jnp.einsum(
        "rs,rt->st", slot_hot, token_hot, preferred_element_type=jnp.float32
    ).astype(jnp.bfloat16)
    experts_ctx = EXPERTS // count_ctx
    share = capacity // slices
    outgoing = jnp.einsum(
        "dct,tf->dcf",
        placement_map.reshape(devices, share, tok_dev),
        moe_in,
        preferred_element_type=jnp.float32,
    ).astype(jnp.bfloat16)
    partner_in = jnp.concatenate([partner_in_low, partner_in_high], axis=1)
    expert_in_both = jnp.concatenate([expert_in, partner_in], axis=0)
    expert_out_both = jnp.concatenate([expert_out, partner_out], axis=0)
    arrived = lax.all_to_all(outgoing, ("ctx", "exp"), split_axis=0, concat_axis=0, tiled=True)
    gate_up = jnp.einsum(
        "dcf,sfh->sdch", arrived, expert_in_both, preferred_element_type=jnp.float32
    )
    activated = (jax.nn.silu(gate_up[..., :ffs_dev]) * gate_up[..., ffs_dev:]).astype(jnp.bfloat16)
    produced = jnp.einsum(
        "sdch,shf->sdcf", activated, expert_out_both, preferred_element_type=jnp.float32
    ).astype(jnp.bfloat16)
    produced = jnp.sum(produced, axis=0, dtype=jnp.float32).astype(jnp.bfloat16)
    returned = lax.all_to_all(produced, ("ctx", "exp"), split_axis=0, concat_axis=0, tiled=True)
    gate_hot = slot_hot.astype(jnp.float32) * gates.reshape(-1)[:, None]
    combiner = jnp.einsum(
        "rs,rt->ts", gate_hot, token_hot.astype(jnp.float32), precision=lax.Precision.HIGHEST
    )
    moe_out = jnp.einsum(
        "tdc,dcf->tf",
        combiner.reshape(tok_dev, devices, share),
        returned.astype(jnp.float32),
        precision=lax.Precision.HIGHEST,
    )
    new_hidden = (residual_mid + moe_out).astype(jnp.bfloat16)
    return (new_hidden, cache)


def solution(mesh):
    in_specs = (
        P(("ctx", "exp"), None),
        P(),
        P(("ctx", "exp"), None),
        P(("ctx", "exp"), None),
        P(),
        P("ctx", "exp"),
        P("ctx", None),
        P(),
        P(),
        P("exp", "ctx"),
        P(),
        P(("ctx", "exp"), None, None),
        P(("ctx", "exp"), None, None),
    )
    out_specs = (P(("ctx", "exp"), None), P(None, "ctx", "exp"))
    return jax.shard_map(shards, mesh=mesh, in_specs=in_specs, out_specs=out_specs, check_vma=False)
```
